32 devices in a mesh: vol: 8 (over z, y), ptcl: 4 (over x, core).
Axes of the slice: x: 2, y: 2, z: 4, core: 2. Of those that a mesh axis runs over, the one named last changes fastest.
Arguments:
- images: bfloat16 [32, 256, 256], P(('vol', 'ptcl')), may hold values from -6 to 6
- defocus: bfloat16 [32], P(('vol', 'ptcl')), may hold values from 20 to 200
- volume: float32 [4096, 256], P('vol'), may hold values from -6 to 6
- counts: int32 [8, 4, 8], P('vol', 'ptcl'), may hold values from 1 to 96, as said below
- slot_pixel: int32 [8, 4, 8, 96], P('vol', 'ptcl'), may hold values from 0 to 511, as said below
- slot_taps: int32 [8, 4, 8, 8, 96], P('vol', 'ptcl'), may hold values from 0 to 511, as said below
- slot_weights: bfloat16 [8, 4, 8, 8, 96], P('vol', 'ptcl'), may hold values from 0.019897461 to 0.25
Outputs:
- volume_next: float32 [4096, 256], P('vol')
The draws below stay inside these ranges and needn't reach their ends.
Inputs may be any that keep to these rules, and one draw needn't show every extreme that they name: The 8 counts of each holder sum to 512; in each particle shard one owner receives exactly 96 live slots from every holder of that shard. `slot_pixel`: the live slots of a holder (slot index below its count) name each of its 512 pixel blocks exactly once; the other slots hold valid ids. `slot_taps`: the 8 taps of one slot name 8 different blocks.
All inputs are finite; a program needn't handle non-finite values.
Results may differ from the reference program's by a relative error of at most 0.0034.
Values may be sent and summed in bfloat16 or wider, within the bound.
No kernel may reach another device: no remote copies, remote signals or barrier semaphores. Data moves between devices by JAX's collectives and lax.ppermute only.
A program may use at most 64 MiB of HBM per device.

```python
import math
import jax
import jax.numpy as jnp
from jax import lax

L = 256
BLK = 128
TAPS = 8
IMG_DEV = 1
BLK_DEV = 512
PB = 512
CAP = 96
IMAGES = 32
VBLOCKS = 4096
N_VOL = 8
N_PTCL = 4


def slot_layout(key):
    pixel_total = IMG_DEV * PB
    key_hot = jax.random.fold_in(key, 71)
    key_jitter = jax.random.fold_in(key, 72)
    key_shuffle = jax.random.fold_in(key, 73)
    remaining = pixel_total - CAP
    base_count = remaining // (N_VOL - 1)
    remainder = remaining % (N_VOL - 1)
    cold_counts = base_count + (jnp.arange(N_VOL - 1) < remainder).astype(jnp.int32)
    jitter = jax.random.randint(key_jitter, (N_VOL, N_PTCL, N_VOL - 1), 0, base_count // 4 + 1)
    cold_counts = cold_counts + jitter - jnp.roll(jitter, 1, axis=2)
    all_counts = jnp.concatenate([jnp.full((N_VOL, N_PTCL, 1), CAP, jnp.int32), cold_counts.astype(jnp.int32)], axis=2)
    hot_owner = jax.random.randint(key_hot, (N_PTCL,), 0, N_VOL)
    place_idx = (jnp.arange(N_VOL)[None, :] - hot_owner[:, None]) % N_VOL
    counts = jnp.take_along_axis(all_counts, jnp.broadcast_to(place_idx[None], all_counts.shape), axis=2)
    scores = jax.random.randint(key_shuffle, (N_VOL, N_PTCL, pixel_total), 0, 65536) * pixel_total + jnp.arange(pixel_total)
    shuffled = jnp.argsort(scores, axis=2).astype(jnp.int32)
    offsets = jnp.cumsum(counts, axis=2) - counts
    position = (offsets[..., None] + jnp.arange(CAP)) % pixel_total
    pixels = jnp.take_along_axis(shuffled, position.reshape(N_VOL, N_PTCL, N_VOL * CAP), axis=2)
    return (counts.astype(jnp.int32), pixels.reshape(N_VOL, N_PTCL, N_VOL, CAP).astype(jnp.int32))


def draw_counts(key, part):
    return slot_layout(key)[0]


def draw_slot_pixel(key, part):
    return slot_layout(key)[1]


def draw_slot_taps(key, part):
    span = BLK_DEV // TAPS
    shape = (N_VOL, N_PTCL, N_VOL, TAPS, CAP)
    key_base = jax.random.fold_in(key, 81)
    key_offset = jax.random.fold_in(key, 82)
    base = jax.random.randint(key_base, (N_VOL, N_PTCL, N_VOL, 1, CAP), 0, BLK_DEV)
    offset = jax.random.randint(key_offset, shape, 0, span)
    tap_ids = jnp.arange(TAPS, dtype=jnp.int32)[None, None, None, :, None]
    first = jnp.zeros(shape, jnp.int32)
    first = first + (jnp.arange(N_VOL)[:, None, None, None, None] == 0).astype(jnp.int32)
    first = first * (jnp.arange(N_PTCL)[None, :, None, None, None] == 0).astype(jnp.int32)
    first = first * (jnp.arange(N_VOL)[None, None, :, None, None] == 0).astype(jnp.int32)
    first = first * (jnp.arange(CAP)[None, None, None, None, :] == 0).astype(jnp.int32)
    forced_offset = jnp.where(tap_ids == TAPS - 1, span - 1, 0)
    base = jnp.where(first > 0, 0, base)
    offset = jnp.where(first > 0, forced_offset, offset)
    return ((base + tap_ids * span + offset) % BLK_DEV).astype(jnp.int32)


def block_levels(rng, dims, shards, low, high):
    level, own = 1.0, jax.random.fold_in(rng, 6)
    for axis_at, shards_of in shards:
        draws = jnp.exp(jax.random.uniform(jax.random.fold_in(own, axis_at), (shards_of,), jnp.float32, low / len(shards), high / len(shards)))
        level = level * jnp.repeat(draws, dims[axis_at] // shards_of).reshape([-1 if axis == axis_at else 1 for axis in range(len(dims))])
    return level


def bell_draw(own_key, extent, spread, limit, cuts=(), kind=jnp.bfloat16):
    array = spread * jax.random.normal(own_key, extent, jnp.float32)
    if cuts:
        array = array * block_levels(own_key, extent, cuts, -0.22, 0.18)
    return jnp.clip(array, -limit, limit).astype(kind)


def setup_inputs(seed: int = 0) -> dict:
    arg_keys = jax.random.split(jax.random.key(seed), 8)
    images = bell_draw(arg_keys[0], (IMAGES, L, L), 1.0, 6.0, ((0, 32),))
    defocus = jnp.clip(jnp.exp(math.log(200.0) - 2.3025851 * jax.random.uniform(arg_keys[1], (IMAGES,), jnp.float32) ** block_levels(arg_keys[1], (IMAGES,), ((0, 32),), -0.2, 0.2)), 20.0, 200.0).astype(jnp.bfloat16)
    volume = bell_draw(arg_keys[2], (VBLOCKS, 2 * BLK), 1.0, 6.0, ((0, 8),), jnp.float32)
    counts = draw_counts(jax.random.fold_in(arg_keys[7], 71), 0)
    slot_pixel = draw_slot_pixel(jax.random.fold_in(arg_keys[7], 71), 0)
    slot_taps = draw_slot_taps(jax.random.fold_in(arg_keys[7], 71), 0)
    slot_weights = jnp.clip(0.019897461 + 0.23010254 * jax.random.uniform(arg_keys[6], (N_VOL, N_PTCL, N_VOL, TAPS, CAP), jnp.float32) ** block_levels(arg_keys[6], (N_VOL, N_PTCL, N_VOL, TAPS, CAP), ((0, 8), (1, 4)), -0.2, 0.2), 0.019897461, 0.25).astype(jnp.bfloat16)
    return dict(images=images, defocus=defocus, volume=volume, counts=counts, slot_pixel=slot_pixel, slot_taps=slot_taps, slot_weights=slot_weights)


learn_rate = 1.0
phase_shift = 0.1


def dft_tables():
    freq_ids = jnp.arange(L, dtype=jnp.int32)
    product = ((freq_ids[:, None] - L // 2) * freq_ids[None, :]) % L
    angle = (2.0 * math.pi / L) * product.astype(jnp.float32)
    return jnp.cos(angle).astype(jnp.bfloat16), jnp.sin(angle).astype(jnp.bfloat16)


def transform(pictures, cos_table, sin_table):
    highest = lax.Precision.HIGHEST
    pixels = pictures.astype(jnp.float32)
    cos_wide = cos_table.astype(jnp.float32)
    sin_wide = sin_table.astype(jnp.float32)
    row_cos = lax.optimization_barrier(jnp.einsum('iyx,kx->iyk', pixels, cos_wide, precision=highest).astype(jnp.bfloat16)).astype(jnp.float32)
    row_sin = lax.optimization_barrier(jnp.einsum('iyx,kx->iyk', pixels, sin_wide, precision=highest).astype(jnp.bfloat16)).astype(jnp.float32)
    real_part = (jnp.einsum('ay,iyb->iab', cos_wide, row_cos, precision=highest) - jnp.einsum('ay,iyb->iab', sin_wide, row_sin, precision=highest)) / L
    imag_part = -(jnp.einsum('ay,iyb->iab', sin_wide, row_cos, precision=highest) + jnp.einsum('ay,iyb->iab', cos_wide, row_sin, precision=highest)) / L
    count_img = pictures.shape[0]
    blocks = jnp.concatenate([real_part.reshape(count_img, PB, BLK), imag_part.reshape(count_img, PB, BLK)], axis=2)
    return blocks.reshape(count_img * PB, 2 * BLK).astype(jnp.bfloat16)


def ctf_rows(pixel_ids, focus):
    block_id = pixel_ids % PB
    row_id = block_id // (L // BLK)
    col_id = (block_id % (L // BLK)) * BLK
    lane_ids = jnp.arange(BLK, dtype=jnp.int32)
    freq_y = (row_id - L // 2).astype(jnp.float32) / L
    freq_x = (col_id[..., None] + lane_ids - L // 2).astype(jnp.float32) / L
    radius = freq_x * freq_x + (freq_y * freq_y)[..., None]
    return -jnp.sin(math.pi * focus.astype(jnp.float32)[..., None] * radius + phase_shift)


def residual_terms(prediction, observed, ctf_values, live_slots):
    shape = prediction.shape
    pred_wide = prediction.astype(jnp.float32).reshape(shape[:-1] + (2, BLK))
    obs_wide = observed.astype(jnp.float32).reshape(shape[:-1] + (2, BLK))
    factor = ctf_values[..., None, :]
    misfit = factor * (factor * pred_wide - obs_wide)
    misfit = jnp.where(live_slots[..., None, None], misfit, 0.0)
    return misfit.reshape(shape).astype(jnp.bfloat16)


def predict_rows(extract, tap_ids, weights):
    summed = jnp.zeros((tap_ids.shape[0], tap_ids.shape[2], extract.shape[1]), jnp.float32)
    for tap_index in range(tap_ids.shape[1]):
        gathered = extract[tap_ids[:, tap_index, :]].astype(jnp.float32)
        summed = summed + weights[:, tap_index, :, None].astype(jnp.float32) * gathered
    return summed


def reference(images, defocus, volume, counts, slot_pixel, slot_taps, slot_weights):
    cos_table, sin_table = dft_tables()
    extract = volume.astype(jnp.bfloat16)
    holders = N_VOL * N_PTCL
    owner_base = (jnp.arange(N_VOL, dtype=jnp.int32) * BLK_DEV)[:, None, None]
    inputs = (images.reshape(holders, IMG_DEV, L, L), defocus.reshape(holders, IMG_DEV),
              counts.reshape(holders, N_VOL), slot_pixel.reshape(holders, N_VOL, CAP),
              slot_taps.reshape(holders, N_VOL, TAPS, CAP), slot_weights.reshape(holders, N_VOL, TAPS, CAP))

    def one_holder(gradient, holder_item):
        pictures, focus_img, slot_count, pixel_ids, tap_ids, weights = holder_item
        observed = transform(pictures, cos_table, sin_table)
        global_ids = (tap_ids + owner_base).astype(jnp.int32)
        prediction = lax.optimization_barrier(predict_rows(extract, global_ids, weights).astype(jnp.bfloat16))
        live_slots = jnp.arange(CAP, dtype=jnp.int32)[None, :] < slot_count[:, None]
        ctf_values = ctf_rows(pixel_ids, focus_img[pixel_ids // PB])
        weighted = residual_terms(prediction, observed[pixel_ids], ctf_values, live_slots).astype(jnp.float32)
        for tap_index in range(TAPS):
            target = global_ids[:, tap_index, :].reshape(-1)
            amount = (weights[:, tap_index, :, None].astype(jnp.float32) * weighted).reshape(-1, 2 * BLK)
            gradient = gradient.at[target].add(amount)
        return gradient, None

    start = jnp.zeros((VBLOCKS, 2 * BLK), jnp.float32)
    gradient = lax.scan(one_holder, start, inputs)[0]
    return volume - learn_rate * gradient
```

```python
import math

import jax
import jax.numpy as jnp
from jax import lax
from jax.sharding import PartitionSpec as P

L = 256
BLK = 128
PB = 512


learn_rate = 1.0
phase_shift = 0.1


def dft_tables():
    freq_ids = jnp.arange(L, dtype=jnp.int32)
    product = (freq_ids[:, None] - L // 2) * freq_ids[None, :] % L
    angle = 2.0 * math.pi / L * product.astype(jnp.float32)
    return (jnp.cos(angle).astype(jnp.bfloat16), jnp.sin(angle).astype(jnp.bfloat16))


def transform(pictures, cos_table, sin_table):
    first = jnp.stack([cos_table, sin_table])
    rows = jnp.einsum(
        "iyx,jkx->ijyk", pictures, first, preferred_element_type=jnp.float32
    ).astype(jnp.bfloat16)
    count_img = pictures.shape[0]
    rows = rows.reshape(count_img, 2 * L, L)
    scale = jnp.asarray(1.0 / L, jnp.bfloat16)
    second = jnp.concatenate(
        [
            jnp.concatenate([cos_table, -sin_table], axis=1),
            jnp.concatenate([-sin_table, -cos_table], axis=1),
        ],
        axis=0,
    ) * scale
    parts = jnp.einsum("ay,iyb->iab", second, rows, preferred_element_type=jnp.float32)
    parts = parts.reshape(count_img, 2, L, L // BLK, BLK)
    blocks = jnp.transpose(parts, (0, 2, 3, 1, 4))
    return blocks.reshape(count_img * PB, 2 * BLK).astype(jnp.bfloat16)


def ctf_rows(block_id, focus):
    row_id = block_id // (L // BLK)
    col_id = block_id % (L // BLK) * BLK
    lane_ids = jnp.arange(BLK, dtype=jnp.int32)
    freq_y = (row_id - L // 2).astype(jnp.float32) / L
    freq_x = (col_id[..., None] + lane_ids - L // 2).astype(jnp.float32) / L
    radius = freq_x * freq_x + (freq_y * freq_y)[..., None]
    return -jnp.sin(math.pi * focus.astype(jnp.float32)[..., None] * radius + phase_shift)


def residual_terms(prediction, observed, ctf_values, live_slots):
    shape = prediction.shape
    pred_wide = prediction.astype(jnp.float32).reshape(shape[:-1] + (2, BLK))
    obs_wide = observed.astype(jnp.float32).reshape(shape[:-1] + (2, BLK))
    factor = ctf_values[..., None, :]
    misfit = factor * (factor * pred_wide - obs_wide)
    misfit = jnp.where(live_slots[..., None, None], misfit, 0.0)
    return misfit.reshape(shape).astype(jnp.bfloat16)


def tap_matrix(tap_ids, weights, block_count):
    owners, taps, slots = tap_ids.shape
    flat_taps = jnp.transpose(tap_ids, (0, 2, 1)).reshape(owners * slots, taps)
    flat_weights = jnp.transpose(weights, (0, 2, 1)).reshape(owners * slots, taps)
    block_ids = jnp.arange(block_count, dtype=jnp.int32)
    picked = jnp.where(
        flat_taps[:, :, None] == block_ids[None, None, :],
        flat_weights[:, :, None],
        jnp.zeros((), jnp.bfloat16),
    )
    return jnp.sum(picked, axis=1, dtype=jnp.bfloat16)


def local(images, defocus, volume, counts, slot_pixel, slot_taps, slot_weights):
    cos_table, sin_table = dft_tables()
    extract = volume.astype(jnp.bfloat16)
    slot_count = counts[0, 0]
    pixel_ids = slot_pixel[0, 0]
    tap_ids = slot_taps[0, 0]
    weights = slot_weights[0, 0]
    owners, taps, capacity = tap_ids.shape
    live_slots = jnp.arange(capacity, dtype=jnp.int32)[None, :] < slot_count[:, None]
    meta = jnp.concatenate(
        [
            tap_ids.astype(jnp.float32),
            weights.astype(jnp.float32),
            (pixel_ids % PB).astype(jnp.float32)[:, None, :],
            defocus[pixel_ids // PB].astype(jnp.float32)[:, None, :],
            live_slots.astype(jnp.float32)[:, None, :],
        ],
        axis=1,
    )
    got_meta = lax.all_to_all(meta, "vol", split_axis=0, concat_axis=0, tiled=True)
    observed = transform(images, cos_table, sin_table)
    rows = observed[pixel_ids]
    got_rows = lax.all_to_all(rows, "vol", split_axis=0, concat_axis=0, tiled=True)
    got_taps = got_meta[:, :taps, :].astype(jnp.int32)
    got_weights = got_meta[:, taps : 2 * taps, :].astype(jnp.bfloat16)
    got_block = got_meta[:, 2 * taps, :].astype(jnp.int32)
    got_focus = got_meta[:, 2 * taps + 1, :]
    got_live = got_meta[:, 2 * taps + 2, :] > 0.5
    matrix = tap_matrix(got_taps, got_weights, volume.shape[0])
    prediction = jnp.dot(matrix, extract, preferred_element_type=jnp.float32)
    prediction = prediction.astype(jnp.bfloat16).reshape(owners, capacity, -1)
    ctf_values = ctf_rows(got_block, got_focus)
    weighted = residual_terms(prediction, got_rows, ctf_values, got_live)
    flat_residual = weighted.reshape(-1, volume.shape[1])
    gradient = lax.dot_general(
        matrix, flat_residual, (((0,), (0,)), ((), ())), preferred_element_type=jnp.float32
    )
    gradient = lax.psum(gradient, "ptcl")
    return volume - learn_rate * gradient


def solution(mesh):
    placed = (
        P(("vol", "ptcl"), None, None),
        P(("vol", "ptcl")),
        P("vol", None),
        P("vol", "ptcl", None),
        P("vol", "ptcl", None, None),
        P("vol", "ptcl", None, None, None),
        P("vol", "ptcl", None, None, None),
    )
    return jax.shard_map(
        local, mesh=mesh, in_specs=placed, out_specs=P("vol", None), check_vma=False
    )
```

```python
import math

import jax
import jax.numpy as jnp
from jax import lax
from jax.sharding import PartitionSpec as P

L = 256
BLK = 128
PB = 512


learn_rate = 1.0
phase_shift = 0.1


def dft_tables():
    freq_ids = jnp.arange(L, dtype=jnp.int32)
    product = (freq_ids[:, None] - L // 2) * freq_ids[None, :] % L
    angle = 2.0 * math.pi / L * product.astype(jnp.float32)
    return (jnp.cos(angle).astype(jnp.bfloat16), jnp.sin(angle).astype(jnp.bfloat16))


def transform(pictures, cos_table, sin_table):
    first = jnp.stack([cos_table, sin_table])
    rows = jnp.einsum(
        "iyx,jkx->ijyk", pictures, first, preferred_element_type=jnp.float32
    ).astype(jnp.bfloat16)
    count_img = pictures.shape[0]
    rows = rows.reshape(count_img, 2 * L, L)
    scale = jnp.asarray(1.0 / L, jnp.bfloat16)
    second = jnp.concatenate(
        [
            jnp.concatenate([cos_table, -sin_table], axis=1),
            jnp.concatenate([-sin_table, -cos_table], axis=1),
        ],
        axis=0,
    ) * scale
    parts = jnp.einsum("ay,iyb->iab", second, rows, preferred_element_type=jnp.float32)
    parts = parts.reshape(count_img, 2, L, L // BLK, BLK)
    blocks = jnp.transpose(parts, (0, 2, 3, 1, 4))
    return blocks.reshape(count_img * PB, 2 * BLK).astype(jnp.bfloat16)


def ctf_rows(block_id, focus):
    row_id = block_id // (L // BLK)
    col_id = block_id % (L // BLK) * BLK
    lane_ids = jnp.arange(BLK, dtype=jnp.int32)
    freq_y = (row_id - L // 2).astype(jnp.float32) / L
    freq_x = (col_id[..., None] + lane_ids - L // 2).astype(jnp.float32) / L
    radius = freq_x * freq_x + (freq_y * freq_y)[..., None]
    return -jnp.sin(math.pi * focus.astype(jnp.float32)[..., None] * radius + phase_shift)


def residual_terms(prediction, observed, ctf_values, live_slots):
    shape = prediction.shape
    pred_wide = prediction.astype(jnp.float32).reshape(shape[:-1] + (2, BLK))
    obs_wide = observed.astype(jnp.float32).reshape(shape[:-1] + (2, BLK))
    factor = ctf_values[..., None, :]
    misfit = factor * (factor * pred_wide - obs_wide)
    misfit = jnp.where(live_slots[..., None, None], misfit, 0.0)
    return misfit.reshape(shape).astype(jnp.bfloat16)


def tap_matrix(tap_ids, weights, block_count):
    owners, taps, slots = tap_ids.shape
    flat_taps = jnp.transpose(tap_ids, (0, 2, 1)).reshape(owners * slots, taps)
    flat_weights = jnp.transpose(weights, (0, 2, 1)).reshape(owners * slots, taps)
    block_ids = jnp.arange(block_count, dtype=jnp.int32)
    picked = jnp.where(
        flat_taps[:, :, None] == block_ids[None, None, :],
        flat_weights[:, :, None],
        jnp.zeros((), jnp.bfloat16),
    )
    return jnp.sum(picked, axis=1, dtype=jnp.bfloat16)


def local(images, defocus, volume, counts, slot_pixel, slot_taps, slot_weights):
    cos_table, sin_table = dft_tables()
    extract = volume.astype(jnp.bfloat16)
    slot_count = counts[0, 0]
    pixel_ids = slot_pixel[0, 0]
    tap_ids = slot_taps[0, 0]
    weights = slot_weights[0, 0]
    owners, taps, capacity = tap_ids.shape
    live_slots = jnp.arange(capacity, dtype=jnp.int32)[None, :] < slot_count[:, None]
    meta = jnp.concatenate(
        [
            tap_ids.astype(jnp.float32),
            weights.astype(jnp.float32),
            (pixel_ids % PB).astype(jnp.float32)[:, None, :],
            defocus[pixel_ids // PB].astype(jnp.float32)[:, None, :],
            live_slots.astype(jnp.float32)[:, None, :],
        ],
        axis=1,
    )
    got_meta = lax.all_to_all(meta, "vol", split_axis=0, concat_axis=0, tiled=True)
    observed = transform(images, cos_table, sin_table)
    rows = observed[pixel_ids]
    got_rows = lax.all_to_all(rows, "vol", split_axis=0, concat_axis=0, tiled=True)
    got_taps = got_meta[:, :taps, :].astype(jnp.int32)
    got_weights = got_meta[:, taps : 2 * taps, :].astype(jnp.bfloat16)
    got_block = got_meta[:, 2 * taps, :].astype(jnp.int32)
    got_focus = got_meta[:, 2 * taps + 1, :]
    got_live = got_meta[:, 2 * taps + 2, :] > 0.5
    matrix = tap_matrix(got_taps, got_weights, volume.shape[0])
    prediction = jnp.dot(matrix, extract, preferred_element_type=jnp.float32)
    prediction = prediction.astype(jnp.bfloat16).reshape(owners, capacity, -1)
    ctf_values = ctf_rows(got_block, got_focus)
    weighted = residual_terms(prediction, got_rows, ctf_values, got_live)
    flat_residual = weighted.reshape(-1, volume.shape[1])
    gradient = lax.dot_general(
        matrix, flat_residual, (((0,), (0,)), ((), ())), preferred_element_type=jnp.float32
    )
    shards = lax.axis_size("ptcl")
    parts = gradient.astype(jnp.bfloat16).reshape(shards, -1, gradient.shape[1])
    got_parts = lax.all_to_all(parts, "ptcl", split_axis=0, concat_axis=0, tiled=True)
    quarter = jnp.sum(got_parts.astype(jnp.float32), axis=0)
    rows_each = quarter.shape[0]
    start = lax.axis_index("ptcl") * rows_each
    mine = lax.dynamic_slice_in_dim(volume, start, rows_each, axis=0)
    updated = mine - learn_rate * quarter
    return lax.all_gather(updated, "ptcl", axis=0, tiled=True)


def solution(mesh):
    placed = (
        P(("vol", "ptcl"), None, None),
        P(("vol", "ptcl")),
        P("vol", None),
        P("vol", "ptcl", None),
        P("vol", "ptcl", None, None),
        P("vol", "ptcl", None, None, None),
        P("vol", "ptcl", None, None, None),
    )
    return jax.shard_map(
        local, mesh=mesh, in_specs=placed, out_specs=P("vol", None), check_vma=False
    )
```

```python
import math

import jax
import jax.numpy as jnp
import ml_dtypes
import numpy as np
from jax import lax
from jax.sharding import PartitionSpec as P

L = 256
BLK = 128
PB = 512


learn_rate = 1.0
phase_shift = 0.1


def dft_tables():
    freq_ids = np.arange(L, dtype=np.int64)
    product = (freq_ids[:, None] - L // 2) * freq_ids[None, :] % L
    angle = np.float32(2.0 * math.pi / L) * product.astype(np.float32)
    cos_table = np.cos(angle.astype(np.float64)).astype(ml_dtypes.bfloat16)
    sin_table = np.sin(angle.astype(np.float64)).astype(ml_dtypes.bfloat16)
    first = np.stack([cos_table, sin_table])
    second = np.concatenate(
        [
            np.concatenate([cos_table, -sin_table], axis=1),
            np.concatenate([-sin_table, -cos_table], axis=1),
        ],
        axis=0,
    ).astype(np.float32) / L
    return first, second.astype(ml_dtypes.bfloat16)


def transform(pictures, first, second):
    rows = jnp.einsum(
        "iyx,jkx->ijyk", pictures, jnp.asarray(first), preferred_element_type=jnp.float32
    ).astype(jnp.bfloat16)
    count_img = pictures.shape[0]
    rows = rows.reshape(count_img, 2 * L, L)
    parts = jnp.einsum(
        "ay,iyb->iab", jnp.asarray(second), rows, preferred_element_type=jnp.float32
    )
    parts = parts.reshape(count_img, 2, L, L // BLK, BLK)
    blocks = jnp.transpose(parts, (0, 2, 3, 1, 4))
    return blocks.reshape(count_img * PB, 2 * BLK).astype(jnp.bfloat16)


def ctf_rows(block_id, focus):
    row_id = block_id // (L // BLK)
    col_id = block_id % (L // BLK) * BLK
    lane_ids = jnp.arange(BLK, dtype=jnp.int32)
    freq_y = (row_id - L // 2).astype(jnp.float32) / L
    freq_x = (col_id[..., None] + lane_ids - L // 2).astype(jnp.float32) / L
    radius = freq_x * freq_x + (freq_y * freq_y)[..., None]
    return -jnp.sin(math.pi * focus.astype(jnp.float32)[..., None] * radius + phase_shift)


def residual_terms(prediction, observed, ctf_values, live_slots):
    shape = prediction.shape
    pred_wide = prediction.astype(jnp.float32).reshape(shape[:-1] + (2, BLK))
    obs_wide = observed.astype(jnp.float32).reshape(shape[:-1] + (2, BLK))
    factor = ctf_values[..., None, :]
    misfit = factor * (factor * pred_wide - obs_wide)
    misfit = jnp.where(live_slots[..., None, None], misfit, 0.0)
    return misfit.reshape(shape).astype(jnp.bfloat16)


def tap_matrix_t(tap_ids, weights, block_count):
    owners, taps, slots = tap_ids.shape
    flat_taps = jnp.transpose(tap_ids, (1, 0, 2)).reshape(taps, owners * slots)
    flat_weights = jnp.transpose(weights, (1, 0, 2)).reshape(taps, owners * slots)
    block_ids = jnp.arange(block_count, dtype=jnp.int32)
    picked = jnp.where(
        flat_taps[:, None, :] == block_ids[None, :, None],
        flat_weights[:, None, :],
        jnp.zeros((), jnp.bfloat16),
    )
    return jnp.sum(picked, axis=0, dtype=jnp.bfloat16)


def split_whole(values):
    return (values // 256).astype(jnp.bfloat16), (values % 256).astype(jnp.bfloat16)


def local(images, defocus, volume, counts, slot_pixel, slot_taps, slot_weights):
    first, second = dft_tables()
    extract = volume.astype(jnp.bfloat16)
    width = volume.shape[1]
    slot_count = counts[0, 0]
    pixel_ids = slot_pixel[0, 0]
    tap_ids = slot_taps[0, 0]
    weights = slot_weights[0, 0]
    owners, taps, capacity = tap_ids.shape
    live_slots = jnp.arange(capacity, dtype=jnp.int32)[None, :] < slot_count[:, None]
    observed = transform(images, first, second)
    flat_pixels = pixel_ids.reshape(-1)
    onehot = (flat_pixels[:, None] == jnp.arange(observed.shape[0], dtype=jnp.int32)[None, :])
    rows = jnp.dot(onehot.astype(jnp.bfloat16), observed, preferred_element_type=jnp.float32)
    rows = rows.astype(jnp.bfloat16).reshape(owners, capacity, width)
    tap_hi, tap_lo = split_whole(tap_ids)
    block_hi, block_lo = split_whole(pixel_ids % PB)
    meta = jnp.concatenate(
        [
            tap_hi,
            tap_lo,
            weights,
            block_hi[:, None, :],
            block_lo[:, None, :],
            defocus[pixel_ids // PB][:, None, :],
            live_slots.astype(jnp.bfloat16)[:, None, :],
        ],
        axis=1,
    )
    fields = meta.shape[1]
    meta_rows = -(-fields * capacity // width)
    flat_meta = meta.reshape(owners, fields * capacity)
    flat_meta = jnp.pad(flat_meta, ((0, 0), (0, meta_rows * width - fields * capacity)))
    packet = jnp.concatenate([rows, flat_meta.reshape(owners, meta_rows, width)], axis=1)
    got = lax.all_to_all(packet, "vol", split_axis=0, concat_axis=0, tiled=True)
    got_rows = got[:, :capacity]
    got_meta = got[:, capacity:].reshape(owners, meta_rows * width)[:, : fields * capacity]
    got_meta = got_meta.reshape(owners, fields, capacity)
    whole = got_meta[:, : 2 * taps].astype(jnp.int32)
    got_taps = whole[:, :taps] * 256 + whole[:, taps:]
    got_weights = got_meta[:, 2 * taps : 3 * taps]
    block_parts = got_meta[:, 3 * taps : 3 * taps + 2].astype(jnp.int32)
    got_block = block_parts[:, 0] * 256 + block_parts[:, 1]
    got_focus = got_meta[:, 3 * taps + 2]
    got_live = got_meta[:, 3 * taps + 3] > 0.5
    matrix_t = tap_matrix_t(got_taps, got_weights, volume.shape[0])
    prediction = lax.dot_general(
        matrix_t, extract, (((0,), (0,)), ((), ())), preferred_element_type=jnp.float32
    )
    prediction = prediction.astype(jnp.bfloat16).reshape(owners, capacity, -1)
    ctf_values = ctf_rows(got_block, got_focus)
    weighted = residual_terms(prediction, got_rows, ctf_values, got_live)
    flat_residual = weighted.reshape(-1, width)
    gradient = jnp.dot(matrix_t, flat_residual, preferred_element_type=jnp.float32)
    shards = lax.axis_size("ptcl")
    parts = gradient.astype(jnp.bfloat16).reshape(shards, -1, gradient.shape[1])
    got_parts = lax.all_to_all(parts, "ptcl", split_axis=0, concat_axis=0, tiled=True)
    quarter = jnp.sum(got_parts.astype(jnp.float32), axis=0)
    rows_each = quarter.shape[0]
    start = lax.axis_index("ptcl") * rows_each
    mine = lax.dynamic_slice_in_dim(volume, start, rows_each, axis=0)
    updated = mine - learn_rate * quarter
    return lax.all_gather(updated, "ptcl", axis=0, tiled=True)


def solution(mesh):
    placed = (
        P(("vol", "ptcl"), None, None),
        P(("vol", "ptcl")),
        P("vol", None),
        P("vol", "ptcl", None),
        P("vol", "ptcl", None, None),
        P("vol", "ptcl", None, None, None),
        P("vol", "ptcl", None, None, None),
    )
    return jax.shard_map(
        local, mesh=mesh, in_specs=placed, out_specs=P("vol", None), check_vma=False
    )
```

```python
import math

import jax
import jax.numpy as jnp
import ml_dtypes
import numpy as np
from jax import lax
from jax.sharding import PartitionSpec as P

L = 256
BLK = 128
PB = 512


learn_rate = 1.0
phase_shift = 0.1


def dft_tables():
    freq_ids = np.arange(L, dtype=np.int64)
    product = (freq_ids[:, None] - L // 2) * freq_ids[None, :] % L
    angle = np.float32(2.0 * math.pi / L) * product.astype(np.float32)
    cos_table = np.cos(angle.astype(np.float64)).astype(ml_dtypes.bfloat16)
    sin_table = np.sin(angle.astype(np.float64)).astype(ml_dtypes.bfloat16)
    first = np.stack([cos_table, sin_table])
    second = np.concatenate(
        [
            np.concatenate([cos_table, -sin_table], axis=1),
            np.concatenate([-sin_table, -cos_table], axis=1),
        ],
        axis=0,
    ).astype(np.float32) / L
    return first, second.astype(ml_dtypes.bfloat16)


def transform(pictures, first, second):
    rows = jnp.einsum(
        "iyx,jkx->ijyk", pictures, jnp.asarray(first), preferred_element_type=jnp.float32
    ).astype(jnp.bfloat16)
    count_img = pictures.shape[0]
    rows = rows.reshape(count_img, 2 * L, L)
    parts = jnp.einsum(
        "ay,iyb->iab", jnp.asarray(second), rows, preferred_element_type=jnp.float32
    )
    parts = parts.reshape(count_img, 2, L, L // BLK, BLK)
    blocks = jnp.transpose(parts, (0, 2, 3, 1, 4))
    return blocks.reshape(count_img * PB, 2 * BLK).astype(jnp.bfloat16)


def ctf_rows(block_id, focus):
    row_id = block_id // (L // BLK)
    col_id = block_id % (L // BLK) * BLK
    lane_ids = jnp.arange(BLK, dtype=jnp.int32)
    freq_y = (row_id - L // 2).astype(jnp.float32) / L
    freq_x = (col_id[..., None] + lane_ids - L // 2).astype(jnp.float32) / L
    radius = freq_x * freq_x + (freq_y * freq_y)[..., None]
    return -jnp.sin(math.pi * focus.astype(jnp.float32)[..., None] * radius + phase_shift)


def residual_terms(prediction, observed, ctf_values, live_slots):
    shape = prediction.shape
    pred_wide = prediction.astype(jnp.float32).reshape(shape[:-1] + (2, BLK))
    obs_wide = observed.astype(jnp.float32).reshape(shape[:-1] + (2, BLK))
    factor = ctf_values[..., None, :]
    misfit = factor * (factor * pred_wide - obs_wide)
    misfit = jnp.where(live_slots[..., None, None], misfit, 0.0)
    return misfit.reshape(shape).astype(jnp.bfloat16)


def tap_matrix_t(tap_ids, weights, block_count):
    owners, taps, slots = tap_ids.shape
    flat_taps = jnp.transpose(tap_ids, (1, 0, 2)).reshape(taps, owners * slots)
    flat_weights = jnp.transpose(weights, (1, 0, 2)).reshape(taps, owners * slots)
    block_ids = jnp.arange(block_count, dtype=jnp.int32)
    picked = jnp.where(
        flat_taps[:, None, :] == block_ids[None, :, None],
        flat_weights[:, None, :],
        jnp.zeros((), jnp.bfloat16),
    )
    return jnp.sum(picked, axis=0, dtype=jnp.bfloat16)


def split_whole(values):
    return (values // 256).astype(jnp.bfloat16), (values % 256).astype(jnp.bfloat16)


def local(images, defocus, volume, counts, slot_pixel, slot_taps, slot_weights):
    first, second = dft_tables()
    extract = volume.astype(jnp.bfloat16)
    width = volume.shape[1]
    slot_count = counts[0, 0]
    pixel_ids = slot_pixel[0, 0]
    tap_ids = slot_taps[0, 0]
    weights = slot_weights[0, 0]
    owners, taps, capacity = tap_ids.shape
    live_slots = jnp.arange(capacity, dtype=jnp.int32)[None, :] < slot_count[:, None]
    tap_hi, tap_lo = split_whole(tap_ids)
    block_hi, block_lo = split_whole(pixel_ids % PB)
    meta = jnp.concatenate(
        [
            tap_hi,
            tap_lo,
            weights,
            block_hi[:, None, :],
            block_lo[:, None, :],
            defocus[pixel_ids // PB][:, None, :],
            live_slots.astype(jnp.bfloat16)[:, None, :],
        ],
        axis=1,
    )
    got_meta = lax.all_to_all(meta, "vol", split_axis=0, concat_axis=0, tiled=True)
    observed = transform(images, first, second)
    flat_pixels = pixel_ids.reshape(-1)
    onehot = (flat_pixels[:, None] == jnp.arange(observed.shape[0], dtype=jnp.int32)[None, :])
    rows = jnp.dot(onehot.astype(jnp.bfloat16), observed, preferred_element_type=jnp.float32)
    rows = rows.astype(jnp.bfloat16).reshape(owners, capacity, width)
    got_rows = lax.all_to_all(rows, "vol", split_axis=0, concat_axis=0, tiled=True)
    whole = got_meta[:, : 2 * taps].astype(jnp.int32)
    got_taps = whole[:, :taps] * 256 + whole[:, taps:]
    got_weights = got_meta[:, 2 * taps : 3 * taps]
    block_parts = got_meta[:, 3 * taps : 3 * taps + 2].astype(jnp.int32)
    got_block = block_parts[:, 0] * 256 + block_parts[:, 1]
    got_focus = got_meta[:, 3 * taps + 2]
    got_live = got_meta[:, 3 * taps + 3] > 0.5
    matrix_t = tap_matrix_t(got_taps, got_weights, volume.shape[0])
    prediction = lax.dot_general(
        matrix_t, extract, (((0,), (0,)), ((), ())), preferred_element_type=jnp.float32
    )
    prediction = prediction.astype(jnp.bfloat16).reshape(owners, capacity, -1)
    ctf_values = ctf_rows(got_block, got_focus)
    weighted = residual_terms(prediction, got_rows, ctf_values, got_live)
    flat_residual = weighted.reshape(-1, width)
    gradient = jnp.dot(matrix_t, flat_residual, preferred_element_type=jnp.float32)
    shards = lax.axis_size("ptcl")
    parts = gradient.astype(jnp.bfloat16).reshape(shards, -1, gradient.shape[1])
    got_parts = lax.all_to_all(parts, "ptcl", split_axis=0, concat_axis=0, tiled=True)
    quarter = jnp.sum(got_parts.astype(jnp.float32), axis=0)
    rows_each = quarter.shape[0]
    start = lax.axis_index("ptcl") * rows_each
    mine = lax.dynamic_slice_in_dim(volume, start, rows_each, axis=0)
    updated = mine - learn_rate * quarter
    return lax.all_gather(updated, "ptcl", axis=0, tiled=True)


def solution(mesh):
    placed = (
        P(("vol", "ptcl"), None, None),
        P(("vol", "ptcl")),
        P("vol", None),
        P("vol", "ptcl", None),
        P("vol", "ptcl", None, None),
        P("vol", "ptcl", None, None, None),
        P("vol", "ptcl", None, None, None),
    )
    return jax.shard_map(
        local, mesh=mesh, in_specs=placed, out_specs=P("vol", None), check_vma=False
    )
```

```python
import math

import jax
import jax.numpy as jnp
import ml_dtypes
import numpy as np
from jax import lax
from jax.sharding import PartitionSpec as P

L = 256
BLK = 128
PB = 512


learn_rate = 1.0
phase_shift = 0.1


def dft_tables():
    freq_ids = np.arange(L, dtype=np.int64)
    product = (freq_ids[:, None] - L // 2) * freq_ids[None, :] % L
    angle = np.float32(2.0 * math.pi / L) * product.astype(np.float32)
    cos_table = np.cos(angle.astype(np.float64)).astype(ml_dtypes.bfloat16)
    sin_table = np.sin(angle.astype(np.float64)).astype(ml_dtypes.bfloat16)
    first = np.stack([cos_table, sin_table])
    second = np.concatenate(
        [
            np.concatenate([cos_table, -sin_table], axis=1),
            np.concatenate([-sin_table, -cos_table], axis=1),
        ],
        axis=0,
    ).astype(np.float32) / L
    return first, second.astype(ml_dtypes.bfloat16)


def transform(pictures, first, second):
    rows = jnp.einsum(
        "iyx,jkx->ijyk", pictures, jnp.asarray(first), preferred_element_type=jnp.float32
    ).astype(jnp.bfloat16)
    count_img = pictures.shape[0]
    rows = rows.reshape(count_img, 2 * L, L)
    parts = jnp.einsum(
        "ay,iyb->iab", jnp.asarray(second), rows, preferred_element_type=jnp.float32
    )
    parts = parts.reshape(count_img, 2, L, L // BLK, BLK)
    blocks = jnp.transpose(parts, (0, 2, 3, 1, 4))
    return blocks.reshape(count_img * PB, 2 * BLK).astype(jnp.bfloat16)


def ctf_rows(block_id, focus):
    row_id = block_id // (L // BLK)
    col_id = block_id % (L // BLK) * BLK
    lane_ids = jnp.arange(BLK, dtype=jnp.int32)
    freq_y = (row_id - L // 2).astype(jnp.float32) / L
    freq_x = (col_id[..., None] + lane_ids - L // 2).astype(jnp.float32) / L
    radius = freq_x * freq_x + (freq_y * freq_y)[..., None]
    return -jnp.sin(math.pi * focus.astype(jnp.float32)[..., None] * radius + phase_shift)


def residual_terms(prediction, observed, ctf_values, live_slots):
    shape = prediction.shape
    pred_wide = prediction.astype(jnp.float32).reshape(shape[:-1] + (2, BLK))
    obs_wide = observed.astype(jnp.float32).reshape(shape[:-1] + (2, BLK))
    factor = ctf_values[..., None, :]
    misfit = factor * (factor * pred_wide - obs_wide)
    misfit = jnp.where(live_slots[..., None, None], misfit, 0.0)
    return misfit.reshape(shape).astype(jnp.bfloat16)


def tap_matrix_t(tap_ids, weights, block_count):
    owners, taps, slots = tap_ids.shape
    flat_taps = jnp.transpose(tap_ids, (1, 0, 2)).reshape(taps, owners * slots)
    flat_weights = jnp.transpose(weights, (1, 0, 2)).reshape(taps, owners * slots)
    block_ids = jnp.arange(block_count, dtype=jnp.int32)
    picked = jnp.where(
        flat_taps[:, None, :] == block_ids[None, :, None],
        flat_weights[:, None, :],
        jnp.zeros((), jnp.bfloat16),
    )
    return jnp.sum(picked, axis=0, dtype=jnp.bfloat16)


def split_whole(values):
    return (values // 256).astype(jnp.bfloat16), (values % 256).astype(jnp.bfloat16)


def local(images, defocus, volume, counts, slot_pixel, slot_taps, slot_weights):
    first, second = dft_tables()
    extract = volume.astype(jnp.bfloat16)
    width = volume.shape[1]
    slot_count = counts[0, 0]
    pixel_ids = slot_pixel[0, 0]
    tap_ids = slot_taps[0, 0]
    weights = slot_weights[0, 0]
    owners, taps, capacity = tap_ids.shape
    live_slots = jnp.arange(capacity, dtype=jnp.int32)[None, :] < slot_count[:, None]
    tap_hi, tap_lo = split_whole(tap_ids)
    block_hi, block_lo = split_whole(pixel_ids % PB)
    pieces = [
        tap_hi,
        tap_lo,
        weights,
        block_hi[:, None, :],
        block_lo[:, None, :],
        defocus[pixel_ids // PB][:, None, :],
        live_slots.astype(jnp.bfloat16)[:, None, :],
    ]
    fields = sum(piece.shape[1] for piece in pieces)
    meta = jnp.zeros((owners, fields, capacity), jnp.bfloat16)
    offset = 0
    for piece in pieces:
        rows_of = piece.shape[1]
        meta = meta + jnp.pad(piece, ((0, 0), (offset, fields - offset - rows_of), (0, 0)))
        offset += rows_of
    got_meta = lax.all_to_all(meta, "vol", split_axis=0, concat_axis=0, tiled=True)
    observed = transform(images, first, second)
    flat_pixels = pixel_ids.reshape(-1)
    onehot = (flat_pixels[:, None] == jnp.arange(observed.shape[0], dtype=jnp.int32)[None, :])
    rows = jnp.dot(onehot.astype(jnp.bfloat16), observed, preferred_element_type=jnp.float32)
    rows = rows.astype(jnp.bfloat16).reshape(owners, capacity, width)
    got_rows = lax.all_to_all(rows, "vol", split_axis=0, concat_axis=0, tiled=True)
    whole = got_meta[:, : 2 * taps].astype(jnp.int32)
    got_taps = whole[:, :taps] * 256 + whole[:, taps:]
    got_weights = got_meta[:, 2 * taps : 3 * taps]
    block_parts = got_meta[:, 3 * taps : 3 * taps + 2].astype(jnp.int32)
    got_block = block_parts[:, 0] * 256 + block_parts[:, 1]
    got_focus = got_meta[:, 3 * taps + 2]
    got_live = got_meta[:, 3 * taps + 3] > 0.5
    matrix_t = tap_matrix_t(got_taps, got_weights, volume.shape[0])
    prediction = lax.dot_general(
        matrix_t, extract, (((0,), (0,)), ((), ())), preferred_element_type=jnp.float32
    )
    prediction = prediction.astype(jnp.bfloat16).reshape(owners, capacity, -1)
    ctf_values = ctf_rows(got_block, got_focus)
    weighted = residual_terms(prediction, got_rows, ctf_values, got_live)
    flat_residual = weighted.reshape(-1, width)
    gradient = jnp.dot(matrix_t, flat_residual, preferred_element_type=jnp.float32)
    shards = lax.axis_size("ptcl")
    parts = gradient.astype(jnp.bfloat16).reshape(shards, -1, gradient.shape[1])
    got_parts = lax.all_to_all(parts, "ptcl", split_axis=0, concat_axis=0, tiled=True)
    quarter = jnp.sum(got_parts.astype(jnp.float32), axis=0)
    rows_each = quarter.shape[0]
    start = lax.axis_index("ptcl") * rows_each
    mine = lax.dynamic_slice_in_dim(volume, start, rows_each, axis=0)
    updated = mine - learn_rate * quarter
    return lax.all_gather(updated, "ptcl", axis=0, tiled=True)


def solution(mesh):
    placed = (
        P(("vol", "ptcl"), None, None),
        P(("vol", "ptcl")),
        P("vol", None),
        P("vol", "ptcl", None),
        P("vol", "ptcl", None, None),
        P("vol", "ptcl", None, None, None),
        P("vol", "ptcl", None, None, None),
    )
    return jax.shard_map(
        local, mesh=mesh, in_specs=placed, out_specs=P("vol", None), check_vma=False
    )
```

```python
import math

import jax
import jax.numpy as jnp
import ml_dtypes
import numpy as np
from jax import lax
from jax.sharding import PartitionSpec as P

L = 256
BLK = 128
PB = 512


learn_rate = 1.0
phase_shift = 0.1


def dft_tables():
    freq_ids = np.arange(L, dtype=np.int64)
    product = (freq_ids[:, None] - L // 2) * freq_ids[None, :] % L
    angle = np.float32(2.0 * math.pi / L) * product.astype(np.float32)
    cos_table = np.cos(angle.astype(np.float64)).astype(ml_dtypes.bfloat16)
    sin_table = np.sin(angle.astype(np.float64)).astype(ml_dtypes.bfloat16)
    first = np.stack([cos_table, sin_table])
    second = np.concatenate(
        [
            np.concatenate([cos_table, -sin_table], axis=1),
            np.concatenate([-sin_table, -cos_table], axis=1),
        ],
        axis=0,
    ).astype(np.float32) / L
    return first, second.astype(ml_dtypes.bfloat16)


def transform(pictures, first, second):
    rows = jnp.einsum(
        "iyx,jkx->ijyk", pictures, jnp.asarray(first), preferred_element_type=jnp.float32
    ).astype(jnp.bfloat16)
    count_img = pictures.shape[0]
    rows = rows.reshape(count_img, 2 * L, L)
    parts = jnp.einsum(
        "ay,iyb->iab", jnp.asarray(second), rows, preferred_element_type=jnp.float32
    )
    parts = parts.reshape(count_img, 2, L, L // BLK, BLK)
    blocks = jnp.transpose(parts, (0, 2, 3, 1, 4))
    return blocks.reshape(count_img * PB, 2 * BLK).astype(jnp.bfloat16)


def ctf_rows(block_id, focus):
    row_id = block_id // (L // BLK)
    col_id = block_id % (L // BLK) * BLK
    lane_ids = jnp.arange(BLK, dtype=jnp.int32)
    freq_y = (row_id - L // 2).astype(jnp.float32) / L
    freq_x = (col_id[..., None] + lane_ids - L // 2).astype(jnp.float32) / L
    radius = freq_x * freq_x + (freq_y * freq_y)[..., None]
    return -jnp.sin(math.pi * focus.astype(jnp.float32)[..., None] * radius + phase_shift)


def residual_terms(prediction, observed, ctf_values, live_slots):
    shape = prediction.shape
    pred_wide = prediction.astype(jnp.float32).reshape(shape[:-1] + (2, BLK))
    obs_wide = observed.astype(jnp.float32).reshape(shape[:-1] + (2, BLK))
    factor = ctf_values[..., None, :]
    misfit = factor * (factor * pred_wide - obs_wide)
    misfit = jnp.where(live_slots[..., None, None], misfit, 0.0)
    return misfit.reshape(shape).astype(jnp.bfloat16)


def tap_matrix_t(tap_ids, weights, block_count):
    owners, taps, slots = tap_ids.shape
    flat_taps = jnp.transpose(tap_ids, (1, 0, 2)).reshape(taps, owners * slots)
    flat_weights = jnp.transpose(weights, (1, 0, 2)).reshape(taps, owners * slots)
    block_ids = jnp.arange(block_count, dtype=jnp.int32)
    picked = jnp.where(
        flat_taps[:, None, :] == block_ids[None, :, None],
        flat_weights[:, None, :],
        jnp.zeros((), jnp.bfloat16),
    )
    return jnp.sum(picked, axis=0, dtype=jnp.bfloat16)


def split_whole(values):
    return (values // 256).astype(jnp.bfloat16), (values % 256).astype(jnp.bfloat16)


def local(images, defocus, volume, counts, slot_pixel, slot_taps, slot_weights):
    first, second = dft_tables()
    extract = volume.astype(jnp.bfloat16)
    width = volume.shape[1]
    slot_count = counts[0, 0]
    pixel_ids = slot_pixel[0, 0]
    tap_ids = slot_taps[0, 0]
    weights = slot_weights[0, 0]
    owners, taps, capacity = tap_ids.shape
    live_slots = jnp.arange(capacity, dtype=jnp.int32)[None, :] < slot_count[:, None]
    tap_hi, tap_lo = split_whole(tap_ids)
    block_hi, block_lo = split_whole(pixel_ids % PB)
    pieces = [
        tap_hi,
        tap_lo,
        weights,
        block_hi[:, None, :],
        block_lo[:, None, :],
        defocus[pixel_ids // PB][:, None, :],
        live_slots.astype(jnp.bfloat16)[:, None, :],
    ]
    fields = sum(piece.shape[1] for piece in pieces)
    meta = jnp.zeros((owners, fields, capacity), jnp.bfloat16)
    offset = 0
    for piece in pieces:
        rows_of = piece.shape[1]
        meta = meta + jnp.pad(piece, ((0, 0), (offset, fields - offset - rows_of), (0, 0)))
        offset += rows_of
    got_meta = lax.all_to_all(meta, "vol", split_axis=0, concat_axis=0, tiled=True)
    observed = transform(images, first, second)
    flat_pixels = pixel_ids.reshape(-1)
    onehot = (flat_pixels[:, None] == jnp.arange(observed.shape[0], dtype=jnp.int32)[None, :])
    rows = jnp.dot(onehot.astype(jnp.bfloat16), observed, preferred_element_type=jnp.float32)
    rows = rows.astype(jnp.bfloat16).reshape(owners, capacity, width)
    got_rows = lax.all_to_all(rows, "vol", split_axis=0, concat_axis=0, tiled=True)
    whole = got_meta[:, : 2 * taps].astype(jnp.int32)
    got_taps = whole[:, :taps] * 256 + whole[:, taps:]
    got_weights = got_meta[:, 2 * taps : 3 * taps]
    block_parts = got_meta[:, 3 * taps : 3 * taps + 2].astype(jnp.int32)
    got_block = block_parts[:, 0] * 256 + block_parts[:, 1]
    got_focus = got_meta[:, 3 * taps + 2]
    got_live = got_meta[:, 3 * taps + 3] > 0.5
    matrix_t = tap_matrix_t(got_taps, got_weights, volume.shape[0])
    prediction = lax.dot_general(
        matrix_t, extract, (((0,), (0,)), ((), ())), preferred_element_type=jnp.float32
    )
    prediction = prediction.astype(jnp.bfloat16).reshape(owners, capacity, -1)
    ctf_values = ctf_rows(got_block, got_focus)
    weighted = residual_terms(prediction, got_rows, ctf_values, got_live)
    flat_residual = weighted.reshape(-1, width)
    gradient = jnp.dot(matrix_t, flat_residual, preferred_element_type=jnp.float32)
    shards = lax.axis_size("ptcl")
    partial = gradient.astype(jnp.bfloat16)
    if shards in (2, 4):
        arrived = [partial.astype(jnp.float32)]
        for shift in range(1, shards):
            pairs = [(i, (i + shift) % shards) for i in range(shards)]
            arrived.append(lax.ppermute(partial, "ptcl", pairs).astype(jnp.float32))
        if shards == 2:
            total = arrived[0] + arrived[1]
        else:
            total = (arrived[0] + arrived[2]) + (arrived[1] + arrived[3])
        return volume - learn_rate * total
    parts = partial.reshape(shards, -1, gradient.shape[1])
    got_parts = lax.all_to_all(parts, "ptcl", split_axis=0, concat_axis=0, tiled=True)
    part_sum = jnp.sum(got_parts.astype(jnp.float32), axis=0)
    rows_each = part_sum.shape[0]
    start = lax.axis_index("ptcl") * rows_each
    mine = lax.dynamic_slice_in_dim(volume, start, rows_each, axis=0)
    updated = mine - learn_rate * part_sum
    return lax.all_gather(updated, "ptcl", axis=0, tiled=True)


def solution(mesh):
    placed = (
        P(("vol", "ptcl"), None, None),
        P(("vol", "ptcl")),
        P("vol", None),
        P("vol", "ptcl", None),
        P("vol", "ptcl", None, None),
        P("vol", "ptcl", None, None, None),
        P("vol", "ptcl", None, None, None),
    )
    return jax.shard_map(
        local, mesh=mesh, in_specs=placed, out_specs=P("vol", None), check_vma=False
    )
```

```python
import math

import jax
import jax.numpy as jnp
import ml_dtypes
import numpy as np
from jax import lax
from jax.sharding import PartitionSpec as P

L = 256
BLK = 128
PB = 512


learn_rate = 1.0
phase_shift = 0.1


def dft_tables():
    freq_ids = np.arange(L, dtype=np.int64)
    product = (freq_ids[:, None] - L // 2) * freq_ids[None, :] % L
    angle = np.float32(2.0 * math.pi / L) * product.astype(np.float32)
    cos_table = np.cos(angle.astype(np.float64)).astype(ml_dtypes.bfloat16)
    sin_table = np.sin(angle.astype(np.float64)).astype(ml_dtypes.bfloat16)
    first = np.stack([cos_table, sin_table])
    second = np.concatenate(
        [
            np.concatenate([cos_table, -sin_table], axis=1),
            np.concatenate([-sin_table, -cos_table], axis=1),
        ],
        axis=0,
    ).astype(np.float32) / L
    return first, second.astype(ml_dtypes.bfloat16)


def transform(pictures, first, second):
    rows = jnp.einsum(
        "iyx,jkx->ijyk", pictures, jnp.asarray(first), preferred_element_type=jnp.float32
    ).astype(jnp.bfloat16)
    count_img = pictures.shape[0]
    rows = rows.reshape(count_img, 2 * L, L)
    parts = jnp.einsum(
        "ay,iyb->iab", jnp.asarray(second), rows, preferred_element_type=jnp.float32
    )
    parts = parts.reshape(count_img, 2, L, L // BLK, BLK)
    blocks = jnp.transpose(parts, (0, 2, 3, 1, 4))
    return blocks.reshape(count_img * PB, 2 * BLK).astype(jnp.bfloat16)


def ctf_rows(block_id, focus):
    row_id = block_id // (L // BLK)
    col_id = block_id % (L // BLK) * BLK
    lane_ids = jnp.arange(BLK, dtype=jnp.int32)
    freq_y = (row_id - L // 2).astype(jnp.float32) / L
    freq_x = (col_id[..., None] + lane_ids - L // 2).astype(jnp.float32) / L
    radius = freq_x * freq_x + (freq_y * freq_y)[..., None]
    return -jnp.sin(math.pi * focus.astype(jnp.float32)[..., None] * radius + phase_shift)


def residual_terms(prediction, observed, ctf_values, live_slots):
    shape = prediction.shape
    pred_wide = prediction.astype(jnp.float32).reshape(shape[:-1] + (2, BLK))
    obs_wide = observed.astype(jnp.float32).reshape(shape[:-1] + (2, BLK))
    factor = ctf_values[..., None, :]
    misfit = factor * (factor * pred_wide - obs_wide)
    misfit = jnp.where(live_slots[..., None, None], misfit, 0.0)
    return misfit.reshape(shape).astype(jnp.bfloat16)


def tap_matrix_t(tap_ids, weights, block_count):
    owners, taps, slots = tap_ids.shape
    flat_taps = jnp.transpose(tap_ids, (1, 0, 2)).reshape(taps, owners * slots)
    flat_weights = jnp.transpose(weights, (1, 0, 2)).reshape(taps, owners * slots)
    block_ids = jnp.arange(block_count, dtype=jnp.int32)
    picked = jnp.where(
        flat_taps[:, None, :] == block_ids[None, :, None],
        flat_weights[:, None, :],
        jnp.zeros((), jnp.bfloat16),
    )
    return jnp.sum(picked, axis=0, dtype=jnp.bfloat16)


def split_whole(values):
    return (values // 256).astype(jnp.bfloat16), (values % 256).astype(jnp.bfloat16)


def exchange(blocks, axis_name):
    count = lax.axis_size(axis_name)
    if count > 8:
        return lax.all_to_all(blocks, axis_name, split_axis=0, concat_axis=0, tiled=True)
    me = lax.axis_index(axis_name)
    arrived = []
    for shift in range(count):
        block = lax.dynamic_index_in_dim(blocks, (me + shift) % count, 0, keepdims=False)
        if shift:
            pairs = [(i, (i + shift) % count) for i in range(count)]
            block = lax.ppermute(block, axis_name, pairs)
        arrived.append(block)
    return jnp.stack(arrived)


def local(images, defocus, volume, counts, slot_pixel, slot_taps, slot_weights):
    first, second = dft_tables()
    extract = volume.astype(jnp.bfloat16)
    width = volume.shape[1]
    slot_count = counts[0, 0]
    pixel_ids = slot_pixel[0, 0]
    tap_ids = slot_taps[0, 0]
    weights = slot_weights[0, 0]
    owners, taps, capacity = tap_ids.shape
    live_slots = jnp.arange(capacity, dtype=jnp.int32)[None, :] < slot_count[:, None]
    tap_hi, tap_lo = split_whole(tap_ids)
    block_hi, block_lo = split_whole(pixel_ids % PB)
    pieces = [
        tap_hi,
        tap_lo,
        weights,
        block_hi[:, None, :],
        block_lo[:, None, :],
        defocus[pixel_ids // PB][:, None, :],
        live_slots.astype(jnp.bfloat16)[:, None, :],
    ]
    fields = sum(piece.shape[1] for piece in pieces)
    meta = jnp.zeros((owners, fields, capacity), jnp.bfloat16)
    offset = 0
    for piece in pieces:
        rows_of = piece.shape[1]
        meta = meta + jnp.pad(piece, ((0, 0), (offset, fields - offset - rows_of), (0, 0)))
        offset += rows_of
    got_meta = exchange(meta, "vol")
    observed = transform(images, first, second)
    flat_pixels = pixel_ids.reshape(-1)
    onehot = (flat_pixels[:, None] == jnp.arange(observed.shape[0], dtype=jnp.int32)[None, :])
    rows = jnp.dot(onehot.astype(jnp.bfloat16), observed, preferred_element_type=jnp.float32)
    rows = rows.astype(jnp.bfloat16).reshape(owners, capacity, width)
    got_rows = exchange(rows, "vol")
    whole = got_meta[:, : 2 * taps].astype(jnp.int32)
    got_taps = whole[:, :taps] * 256 + whole[:, taps:]
    got_weights = got_meta[:, 2 * taps : 3 * taps]
    block_parts = got_meta[:, 3 * taps : 3 * taps + 2].astype(jnp.int32)
    got_block = block_parts[:, 0] * 256 + block_parts[:, 1]
    got_focus = got_meta[:, 3 * taps + 2]
    got_live = got_meta[:, 3 * taps + 3] > 0.5
    matrix_t = tap_matrix_t(got_taps, got_weights, volume.shape[0])
    prediction = lax.dot_general(
        matrix_t, extract, (((0,), (0,)), ((), ())), preferred_element_type=jnp.float32
    )
    prediction = prediction.astype(jnp.bfloat16).reshape(owners, capacity, -1)
    ctf_values = ctf_rows(got_block, got_focus)
    weighted = residual_terms(prediction, got_rows, ctf_values, got_live)
    flat_residual = weighted.reshape(-1, width)
    gradient = jnp.dot(matrix_t, flat_residual, preferred_element_type=jnp.float32)
    shards = lax.axis_size("ptcl")
    partial = gradient.astype(jnp.bfloat16)
    if shards in (2, 4):
        arrived = [partial.astype(jnp.float32)]
        for shift in range(1, shards):
            pairs = [(i, (i + shift) % shards) for i in range(shards)]
            arrived.append(lax.ppermute(partial, "ptcl", pairs).astype(jnp.float32))
        if shards == 2:
            total = arrived[0] + arrived[1]
        else:
            total = (arrived[0] + arrived[2]) + (arrived[1] + arrived[3])
        return volume - learn_rate * total
    parts = partial.reshape(shards, -1, gradient.shape[1])
    got_parts = lax.all_to_all(parts, "ptcl", split_axis=0, concat_axis=0, tiled=True)
    part_sum = jnp.sum(got_parts.astype(jnp.float32), axis=0)
    rows_each = part_sum.shape[0]
    start = lax.axis_index("ptcl") * rows_each
    mine = lax.dynamic_slice_in_dim(volume, start, rows_each, axis=0)
    updated = mine - learn_rate * part_sum
    return lax.all_gather(updated, "ptcl", axis=0, tiled=True)


def solution(mesh):
    placed = (
        P(("vol", "ptcl"), None, None),
        P(("vol", "ptcl")),
        P("vol", None),
        P("vol", "ptcl", None),
        P("vol", "ptcl", None, None),
        P("vol", "ptcl", None, None, None),
        P("vol", "ptcl", None, None, None),
    )
    return jax.shard_map(
        local, mesh=mesh, in_specs=placed, out_specs=P("vol", None), check_vma=False
    )
```

```python
import math

import jax
import jax.numpy as jnp
import ml_dtypes
import numpy as np
from jax import lax
from jax.sharding import PartitionSpec as P

L = 256
BLK = 128
PB = 512


learn_rate = 1.0
phase_shift = 0.1


def dft_tables():
    freq_ids = np.arange(L, dtype=np.int64)
    product = (freq_ids[:, None] - L // 2) * freq_ids[None, :] % L
    angle = np.float32(2.0 * math.pi / L) * product.astype(np.float32)
    cos_table = np.cos(angle.astype(np.float64)).astype(ml_dtypes.bfloat16)
    sin_table = np.sin(angle.astype(np.float64)).astype(ml_dtypes.bfloat16)
    first = np.stack([cos_table, sin_table])
    second = np.concatenate(
        [
            np.concatenate([cos_table, -sin_table], axis=1),
            np.concatenate([-sin_table, -cos_table], axis=1),
        ],
        axis=0,
    ).astype(np.float32) / L
    return first, second.astype(ml_dtypes.bfloat16)


def transform(pictures, first, second):
    rows = jnp.einsum(
        "iyx,jkx->ijyk", pictures, jnp.asarray(first), preferred_element_type=jnp.float32
    ).astype(jnp.bfloat16)
    count_img = pictures.shape[0]
    rows = rows.reshape(count_img, 2 * L, L)
    parts = jnp.einsum(
        "ay,iyb->iab", jnp.asarray(second), rows, preferred_element_type=jnp.float32
    )
    parts = parts.reshape(count_img, 2, L, L // BLK, BLK)
    blocks = jnp.transpose(parts, (0, 2, 3, 1, 4))
    return blocks.reshape(count_img * PB, 2 * BLK).astype(jnp.bfloat16)


def ctf_rows(block_id, focus):
    row_id = block_id // (L // BLK)
    col_id = block_id % (L // BLK) * BLK
    lane_ids = jnp.arange(BLK, dtype=jnp.int32)
    freq_y = (row_id - L // 2).astype(jnp.float32) / L
    freq_x = (col_id[..., None] + lane_ids - L // 2).astype(jnp.float32) / L
    radius = freq_x * freq_x + (freq_y * freq_y)[..., None]
    return -jnp.sin(math.pi * focus.astype(jnp.float32)[..., None] * radius + phase_shift)


def residual_terms(prediction, observed, ctf_values, live_slots):
    shape = prediction.shape
    pred_wide = prediction.astype(jnp.float32).reshape(shape[:-1] + (2, BLK))
    obs_wide = observed.astype(jnp.float32).reshape(shape[:-1] + (2, BLK))
    factor = ctf_values[..., None, :]
    misfit = factor * (factor * pred_wide - obs_wide)
    misfit = jnp.where(live_slots[..., None, None], misfit, 0.0)
    return misfit.reshape(shape).astype(jnp.bfloat16)


def tap_matrix_t(tap_ids, weights, block_count):
    owners, taps, slots = tap_ids.shape
    flat_taps = jnp.transpose(tap_ids, (1, 0, 2)).reshape(taps, owners * slots)
    flat_weights = jnp.transpose(weights, (1, 0, 2)).reshape(taps, owners * slots)
    block_ids = jnp.arange(block_count, dtype=jnp.int32)
    picked = jnp.where(
        flat_taps[:, None, :] == block_ids[None, :, None],
        flat_weights[:, None, :],
        jnp.zeros((), jnp.bfloat16),
    )
    return jnp.sum(picked, axis=0, dtype=jnp.bfloat16)


def split_whole(values):
    return (values // 256).astype(jnp.bfloat16), (values % 256).astype(jnp.bfloat16)


def local(images, defocus, volume, counts, slot_pixel, slot_taps, slot_weights):
    first, second = dft_tables()
    extract = volume.astype(jnp.bfloat16)
    width = volume.shape[1]
    slot_count = counts[0, 0]
    pixel_ids = slot_pixel[0, 0]
    tap_ids = slot_taps[0, 0]
    weights = slot_weights[0, 0]
    owners, taps, capacity = tap_ids.shape
    live_slots = jnp.arange(capacity, dtype=jnp.int32)[None, :] < slot_count[:, None]
    tap_hi, tap_lo = split_whole(tap_ids)
    block_hi, block_lo = split_whole(pixel_ids % PB)
    pieces = [
        tap_hi,
        tap_lo,
        weights,
        block_hi[:, None, :],
        block_lo[:, None, :],
        defocus[pixel_ids // PB][:, None, :],
        live_slots.astype(jnp.bfloat16)[:, None, :],
    ]
    fields = sum(piece.shape[1] for piece in pieces)
    meta = jnp.zeros((owners, fields, capacity), jnp.bfloat16)
    offset = 0
    for piece in pieces:
        rows_of = piece.shape[1]
        meta = meta + jnp.pad(piece, ((0, 0), (offset, fields - offset - rows_of), (0, 0)))
        offset += rows_of
    got_meta = lax.all_to_all(meta, "vol", split_axis=0, concat_axis=0, tiled=True)
    observed = transform(images, first, second)
    flat_pixels = pixel_ids.reshape(-1)
    onehot = (flat_pixels[:, None] == jnp.arange(observed.shape[0], dtype=jnp.int32)[None, :])
    rows = jnp.dot(onehot.astype(jnp.bfloat16), observed, preferred_element_type=jnp.float32)
    rows = rows.astype(jnp.bfloat16).reshape(owners, capacity, width)
    got_rows = lax.all_to_all(rows, "vol", split_axis=0, concat_axis=0, tiled=True)
    whole = got_meta[:, : 2 * taps].astype(jnp.int32)
    got_taps = whole[:, :taps] * 256 + whole[:, taps:]
    got_weights = got_meta[:, 2 * taps : 3 * taps]
    block_parts = got_meta[:, 3 * taps : 3 * taps + 2].astype(jnp.int32)
    got_block = block_parts[:, 0] * 256 + block_parts[:, 1]
    got_focus = got_meta[:, 3 * taps + 2]
    got_live = got_meta[:, 3 * taps + 3] > 0.5
    matrix_t = tap_matrix_t(got_taps, got_weights, volume.shape[0])
    prediction = lax.dot_general(
        matrix_t, extract, (((0,), (0,)), ((), ())), preferred_element_type=jnp.float32
    )
    prediction = prediction.astype(jnp.bfloat16).reshape(owners, capacity, -1)
    ctf_values = ctf_rows(got_block, got_focus)
    weighted = residual_terms(prediction, got_rows, ctf_values, got_live)
    flat_residual = weighted.reshape(-1, width)
    gradient = jnp.dot(matrix_t, flat_residual, preferred_element_type=jnp.float32)
    shards = lax.axis_size("ptcl")
    if shards == 4:
        me = lax.axis_index("ptcl")
        on_chip = [(i, i ^ 1) for i in range(shards)]
        across = [(i, i ^ 2) for i in range(shards)]
        pair_sum = gradient + lax.ppermute(gradient, "ptcl", on_chip)
        half = gradient.shape[0] // 2
        core = me % 2
        mine = lax.dynamic_slice_in_dim(pair_sum, core * half, half, axis=0)
        total = mine + lax.ppermute(mine, "ptcl", across)
        updated = lax.dynamic_slice_in_dim(volume, core * half, half, axis=0) - learn_rate * total
        other = lax.ppermute(updated, "ptcl", on_chip)
        return jnp.where(
            core == 0,
            jnp.concatenate([updated, other], axis=0),
            jnp.concatenate([other, updated], axis=0),
        )
    partial = gradient.astype(jnp.bfloat16)
    parts = partial.reshape(shards, -1, gradient.shape[1])
    got_parts = lax.all_to_all(parts, "ptcl", split_axis=0, concat_axis=0, tiled=True)
    part_sum = jnp.sum(got_parts.astype(jnp.float32), axis=0)
    rows_each = part_sum.shape[0]
    start = lax.axis_index("ptcl") * rows_each
    mine = lax.dynamic_slice_in_dim(volume, start, rows_each, axis=0)
    updated = mine - learn_rate * part_sum
    return lax.all_gather(updated, "ptcl", axis=0, tiled=True)


def solution(mesh):
    placed = (
        P(("vol", "ptcl"), None, None),
        P(("vol", "ptcl")),
        P("vol", None),
        P("vol", "ptcl", None),
        P("vol", "ptcl", None, None),
        P("vol", "ptcl", None, None, None),
        P("vol", "ptcl", None, None, None),
    )
    return jax.shard_map(
        local, mesh=mesh, in_specs=placed, out_specs=P("vol", None), check_vma=False
    )
```

```python
import math

import jax
import jax.numpy as jnp
import ml_dtypes
import numpy as np
from jax import lax
from jax.sharding import PartitionSpec as P

L = 256
BLK = 128
PB = 512


learn_rate = 1.0
phase_shift = 0.1


def dft_tables():
    freq_ids = np.arange(L, dtype=np.int64)
    product = (freq_ids[:, None] - L // 2) * freq_ids[None, :] % L
    angle = np.float32(2.0 * math.pi / L) * product.astype(np.float32)
    cos_table = np.cos(angle.astype(np.float64)).astype(ml_dtypes.bfloat16)
    sin_table = np.sin(angle.astype(np.float64)).astype(ml_dtypes.bfloat16)
    first = np.stack([cos_table, sin_table])
    second = np.concatenate(
        [
            np.concatenate([cos_table, -sin_table], axis=1),
            np.concatenate([-sin_table, -cos_table], axis=1),
        ],
        axis=0,
    ).astype(np.float32) / L
    return first, second.astype(ml_dtypes.bfloat16)


def transform(pictures, first, second):
    rows = jnp.einsum(
        "iyx,jkx->ijyk", pictures, jnp.asarray(first), preferred_element_type=jnp.float32
    ).astype(jnp.bfloat16)
    count_img = pictures.shape[0]
    rows = rows.reshape(count_img, 2 * L, L)
    parts = jnp.einsum(
        "ay,iyb->iab", jnp.asarray(second), rows, preferred_element_type=jnp.float32
    )
    parts = parts.reshape(count_img, 2, L, L // BLK, BLK)
    blocks = jnp.transpose(parts, (0, 2, 3, 1, 4))
    return blocks.reshape(count_img * PB, 2 * BLK).astype(jnp.bfloat16)


def ctf_rows(block_id, focus):
    row_id = block_id // (L // BLK)
    col_id = block_id % (L // BLK) * BLK
    lane_ids = jnp.arange(BLK, dtype=jnp.int32)
    freq_y = (row_id - L // 2).astype(jnp.float32) / L
    freq_x = (col_id[..., None] + lane_ids - L // 2).astype(jnp.float32) / L
    radius = freq_x * freq_x + (freq_y * freq_y)[..., None]
    return -jnp.sin(math.pi * focus.astype(jnp.float32)[..., None] * radius + phase_shift)


def residual_terms(prediction, observed, ctf_values, live_slots):
    shape = prediction.shape
    pred_wide = prediction.astype(jnp.float32).reshape(shape[:-1] + (2, BLK))
    obs_wide = observed.astype(jnp.float32).reshape(shape[:-1] + (2, BLK))
    factor = ctf_values[..., None, :]
    misfit = factor * (factor * pred_wide - obs_wide)
    misfit = jnp.where(live_slots[..., None, None], misfit, 0.0)
    return misfit.reshape(shape).astype(jnp.bfloat16)


def tap_matrix_t(tap_ids, weights, block_count):
    owners, taps, slots = tap_ids.shape
    flat_taps = jnp.transpose(tap_ids, (1, 0, 2)).reshape(taps, owners * slots)
    flat_weights = jnp.transpose(weights, (1, 0, 2)).reshape(taps, owners * slots)
    block_ids = jnp.arange(block_count, dtype=jnp.int32)
    picked = jnp.where(
        flat_taps[:, None, :] == block_ids[None, :, None],
        flat_weights[:, None, :],
        jnp.zeros((), jnp.bfloat16),
    )
    return jnp.sum(picked, axis=0, dtype=jnp.bfloat16)


def split_whole(values):
    return (values // 256).astype(jnp.bfloat16), (values % 256).astype(jnp.bfloat16)


def local(images, defocus, volume, counts, slot_pixel, slot_taps, slot_weights):
    first, second = dft_tables()
    extract = volume.astype(jnp.bfloat16)
    width = volume.shape[1]
    slot_count = counts[0, 0]
    pixel_ids = slot_pixel[0, 0]
    tap_ids = slot_taps[0, 0]
    weights = slot_weights[0, 0]
    owners, taps, capacity = tap_ids.shape
    live_slots = jnp.arange(capacity, dtype=jnp.int32)[None, :] < slot_count[:, None]
    tap_hi, tap_lo = split_whole(tap_ids)
    block_hi, block_lo = split_whole(pixel_ids % PB)
    pieces = [
        tap_hi,
        tap_lo,
        weights,
        block_hi[:, None, :],
        block_lo[:, None, :],
        defocus[pixel_ids // PB][:, None, :],
        live_slots.astype(jnp.bfloat16)[:, None, :],
    ]
    fields = sum(piece.shape[1] for piece in pieces)
    meta = jnp.zeros((owners, fields, capacity), jnp.bfloat16)
    offset = 0
    for piece in pieces:
        rows_of = piece.shape[1]
        meta = meta + jnp.pad(piece, ((0, 0), (offset, fields - offset - rows_of), (0, 0)))
        offset += rows_of
    got_meta = lax.all_to_all(meta, "vol", split_axis=0, concat_axis=0, tiled=True)
    observed = transform(images, first, second)
    flat_pixels = pixel_ids.reshape(-1)
    onehot = (flat_pixels[:, None] == jnp.arange(observed.shape[0], dtype=jnp.int32)[None, :])
    rows = jnp.dot(onehot.astype(jnp.bfloat16), observed, preferred_element_type=jnp.float32)
    rows = rows.astype(jnp.bfloat16).reshape(owners, capacity, width)
    got_rows = lax.all_to_all(rows, "vol", split_axis=0, concat_axis=0, tiled=True)
    whole = got_meta[:, : 2 * taps].astype(jnp.int32)
    got_taps = whole[:, :taps] * 256 + whole[:, taps:]
    got_weights = got_meta[:, 2 * taps : 3 * taps]
    block_parts = got_meta[:, 3 * taps : 3 * taps + 2].astype(jnp.int32)
    got_block = block_parts[:, 0] * 256 + block_parts[:, 1]
    got_focus = got_meta[:, 3 * taps + 2]
    got_live = got_meta[:, 3 * taps + 3] > 0.5
    matrix_t = tap_matrix_t(got_taps, got_weights, volume.shape[0])
    prediction = lax.dot_general(
        matrix_t, extract, (((0,), (0,)), ((), ())), preferred_element_type=jnp.float32
    )
    prediction = prediction.astype(jnp.bfloat16).reshape(owners, capacity, -1)
    ctf_values = ctf_rows(got_block, got_focus)
    weighted = residual_terms(prediction, got_rows, ctf_values, got_live)
    flat_residual = weighted.reshape(-1, width)
    gradient = jnp.dot(matrix_t, flat_residual, preferred_element_type=jnp.float32)
    shards = lax.axis_size("ptcl")
    if shards == 4:
        me = lax.axis_index("ptcl")
        on_chip = [(i, i ^ 1) for i in range(shards)]
        across = [(i, i ^ 2) for i in range(shards)]
        pair_sum = gradient + lax.ppermute(gradient, "ptcl", on_chip)
        half = gradient.shape[0] // 2
        core = me % 2
        mine = lax.dynamic_slice_in_dim(pair_sum, core * half, half, axis=0).astype(jnp.bfloat16)
        total = mine.astype(jnp.float32) + lax.ppermute(mine, "ptcl", across).astype(jnp.float32)
        updated = lax.dynamic_slice_in_dim(volume, core * half, half, axis=0) - learn_rate * total
        other = lax.ppermute(updated, "ptcl", on_chip)
        return jnp.where(
            core == 0,
            jnp.concatenate([updated, other], axis=0),
            jnp.concatenate([other, updated], axis=0),
        )
    partial = gradient.astype(jnp.bfloat16)
    parts = partial.reshape(shards, -1, gradient.shape[1])
    got_parts = lax.all_to_all(parts, "ptcl", split_axis=0, concat_axis=0, tiled=True)
    part_sum = jnp.sum(got_parts.astype(jnp.float32), axis=0)
    rows_each = part_sum.shape[0]
    start = lax.axis_index("ptcl") * rows_each
    mine = lax.dynamic_slice_in_dim(volume, start, rows_each, axis=0)
    updated = mine - learn_rate * part_sum
    return lax.all_gather(updated, "ptcl", axis=0, tiled=True)


def solution(mesh):
    placed = (
        P(("vol", "ptcl"), None, None),
        P(("vol", "ptcl")),
        P("vol", None),
        P("vol", "ptcl", None),
        P("vol", "ptcl", None, None),
        P("vol", "ptcl", None, None, None),
        P("vol", "ptcl", None, None, None),
    )
    return jax.shard_map(
        local, mesh=mesh, in_specs=placed, out_specs=P("vol", None), check_vma=False
    )
```

```python
import math

import jax
import jax.numpy as jnp
import ml_dtypes
import numpy as np
from jax import lax
from jax.sharding import PartitionSpec as P

L = 256
BLK = 128
PB = 512


learn_rate = 1.0
phase_shift = 0.1


def dft_tables():
    freq_ids = np.arange(L, dtype=np.int64)
    product = (freq_ids[:, None] - L // 2) * freq_ids[None, :] % L
    angle = np.float32(2.0 * math.pi / L) * product.astype(np.float32)
    cos_table = np.cos(angle.astype(np.float64)).astype(ml_dtypes.bfloat16)
    sin_table = np.sin(angle.astype(np.float64)).astype(ml_dtypes.bfloat16)
    first = np.stack([cos_table, sin_table])
    second = np.concatenate(
        [
            np.concatenate([cos_table, -sin_table], axis=1),
            np.concatenate([-sin_table, -cos_table], axis=1),
        ],
        axis=0,
    ).astype(np.float32) / L
    return first, second.astype(ml_dtypes.bfloat16)


def transform(pictures, first, second):
    rows = jnp.einsum(
        "iyx,jkx->ijyk", pictures, jnp.asarray(first), preferred_element_type=jnp.float32
    ).astype(jnp.bfloat16)
    count_img = pictures.shape[0]
    rows = rows.reshape(count_img, 2 * L, L)
    parts = jnp.einsum(
        "ay,iyb->iab", jnp.asarray(second), rows, preferred_element_type=jnp.float32
    )
    parts = parts.reshape(count_img, 2, L, L // BLK, BLK)
    blocks = jnp.transpose(parts, (0, 2, 3, 1, 4))
    return blocks.reshape(count_img * PB, 2 * BLK).astype(jnp.bfloat16)


def ctf_rows(block_id, focus):
    row_id = block_id // (L // BLK)
    col_id = block_id % (L // BLK) * BLK
    lane_ids = jnp.arange(BLK, dtype=jnp.int32)
    freq_y = (row_id - L // 2).astype(jnp.float32) / L
    freq_x = (col_id[..., None] + lane_ids - L // 2).astype(jnp.float32) / L
    radius = freq_x * freq_x + (freq_y * freq_y)[..., None]
    return -jnp.sin(math.pi * focus.astype(jnp.float32)[..., None] * radius + phase_shift)


def residual_terms(prediction, observed, ctf_values, live_slots):
    shape = prediction.shape
    pred_wide = prediction.astype(jnp.float32).reshape(shape[:-1] + (2, BLK))
    obs_wide = observed.astype(jnp.float32).reshape(shape[:-1] + (2, BLK))
    factor = ctf_values[..., None, :]
    misfit = factor * (factor * pred_wide - obs_wide)
    misfit = jnp.where(live_slots[..., None, None], misfit, 0.0)
    return misfit.reshape(shape).astype(jnp.bfloat16)


def tap_matrix_t(tap_ids, weights, block_count):
    owners, taps, slots = tap_ids.shape
    flat_taps = jnp.transpose(tap_ids, (1, 0, 2)).reshape(taps, owners * slots)
    flat_weights = jnp.transpose(weights, (1, 0, 2)).reshape(taps, owners * slots)
    block_ids = jnp.arange(block_count, dtype=jnp.int32)
    picked = jnp.where(
        flat_taps[:, None, :] == block_ids[None, :, None],
        flat_weights[:, None, :],
        jnp.zeros((), jnp.bfloat16),
    )
    return jnp.sum(picked, axis=0, dtype=jnp.bfloat16)


def split_whole(values):
    return (values // 256).astype(jnp.bfloat16), (values % 256).astype(jnp.bfloat16)


def local(images, defocus, volume, counts, slot_pixel, slot_taps, slot_weights):
    first, second = dft_tables()
    extract = volume.astype(jnp.bfloat16)
    width = volume.shape[1]
    slot_count = counts[0, 0]
    pixel_ids = slot_pixel[0, 0]
    tap_ids = slot_taps[0, 0]
    weights = slot_weights[0, 0]
    owners, taps, capacity = tap_ids.shape
    live_slots = jnp.arange(capacity, dtype=jnp.int32)[None, :] < slot_count[:, None]
    tap_hi, tap_lo = split_whole(tap_ids)
    block_hi, block_lo = split_whole(pixel_ids % PB)
    pieces = [
        tap_hi,
        tap_lo,
        weights,
        block_hi[:, None, :],
        block_lo[:, None, :],
        defocus[pixel_ids // PB][:, None, :],
        live_slots.astype(jnp.bfloat16)[:, None, :],
    ]
    fields = sum(piece.shape[1] for piece in pieces)
    meta = jnp.zeros((owners, fields, capacity), jnp.bfloat16)
    offset = 0
    for piece in pieces:
        rows_of = piece.shape[1]
        meta = meta + jnp.pad(piece, ((0, 0), (offset, fields - offset - rows_of), (0, 0)))
        offset += rows_of
    observed = transform(images, first, second)
    flat_pixels = pixel_ids.reshape(-1)
    onehot = (flat_pixels[:, None] == jnp.arange(observed.shape[0], dtype=jnp.int32)[None, :])
    rows = jnp.dot(onehot.astype(jnp.bfloat16), observed, preferred_element_type=jnp.float32)
    rows = rows.astype(jnp.bfloat16).reshape(owners, capacity, width)
    meta_rows = -(-fields * capacity // width)
    flat_meta = meta.reshape(owners, fields * capacity)
    flat_meta = jnp.pad(flat_meta, ((0, 0), (0, meta_rows * width - fields * capacity)))
    packet = jnp.concatenate([rows, flat_meta.reshape(owners, meta_rows, width)], axis=1)
    got = lax.all_to_all(packet, "vol", split_axis=0, concat_axis=0, tiled=True)
    extract = lax.optimization_barrier(extract)
    got_rows = got[:, :capacity]
    got_meta = got[:, capacity:].reshape(owners, meta_rows * width)[:, : fields * capacity]
    got_meta = got_meta.reshape(owners, fields, capacity)
    whole = got_meta[:, : 2 * taps].astype(jnp.int32)
    got_taps = whole[:, :taps] * 256 + whole[:, taps:]
    got_weights = got_meta[:, 2 * taps : 3 * taps]
    block_parts = got_meta[:, 3 * taps : 3 * taps + 2].astype(jnp.int32)
    got_block = block_parts[:, 0] * 256 + block_parts[:, 1]
    got_focus = got_meta[:, 3 * taps + 2]
    got_live = got_meta[:, 3 * taps + 3] > 0.5
    matrix_t = tap_matrix_t(got_taps, got_weights, volume.shape[0])
    prediction = lax.dot_general(
        matrix_t, extract, (((0,), (0,)), ((), ())), preferred_element_type=jnp.float32
    )
    prediction = prediction.astype(jnp.bfloat16).reshape(owners, capacity, -1)
    ctf_values = ctf_rows(got_block, got_focus)
    weighted = residual_terms(prediction, got_rows, ctf_values, got_live)
    flat_residual = weighted.reshape(-1, width)
    gradient = jnp.dot(matrix_t, flat_residual, preferred_element_type=jnp.float32)
    shards = lax.axis_size("ptcl")
    if shards == 4:
        me = lax.axis_index("ptcl")
        on_chip = [(i, i ^ 1) for i in range(shards)]
        across = [(i, i ^ 2) for i in range(shards)]
        pair_sum = gradient + lax.ppermute(gradient, "ptcl", on_chip)
        half = gradient.shape[0] // 2
        core = me % 2
        mine = lax.dynamic_slice_in_dim(pair_sum, core * half, half, axis=0).astype(jnp.bfloat16)
        total = mine.astype(jnp.float32) + lax.ppermute(mine, "ptcl", across).astype(jnp.float32)
        updated = lax.dynamic_slice_in_dim(volume, core * half, half, axis=0) - learn_rate * total
        other = lax.ppermute(updated, "ptcl", on_chip)
        return jnp.where(
            core == 0,
            jnp.concatenate([updated, other], axis=0),
            jnp.concatenate([other, updated], axis=0),
        )
    partial = gradient.astype(jnp.bfloat16)
    parts = partial.reshape(shards, -1, gradient.shape[1])
    got_parts = lax.all_to_all(parts, "ptcl", split_axis=0, concat_axis=0, tiled=True)
    part_sum = jnp.sum(got_parts.astype(jnp.float32), axis=0)
    rows_each = part_sum.shape[0]
    start = lax.axis_index("ptcl") * rows_each
    mine = lax.dynamic_slice_in_dim(volume, start, rows_each, axis=0)
    updated = mine - learn_rate * part_sum
    return lax.all_gather(updated, "ptcl", axis=0, tiled=True)


def solution(mesh):
    placed = (
        P(("vol", "ptcl"), None, None),
        P(("vol", "ptcl")),
        P("vol", None),
        P("vol", "ptcl", None),
        P("vol", "ptcl", None, None),
        P("vol", "ptcl", None, None, None),
        P("vol", "ptcl", None, None, None),
    )
    return jax.shard_map(
        local, mesh=mesh, in_specs=placed, out_specs=P("vol", None), check_vma=False
    )
```

```python
import math

import jax
import jax.numpy as jnp
import ml_dtypes
import numpy as np
from jax import lax
from jax.sharding import PartitionSpec as P

L = 256
BLK = 128
PB = 512


learn_rate = 1.0
phase_shift = 0.1


def dft_tables():
    freq_ids = np.arange(L, dtype=np.int64)
    product = (freq_ids[:, None] - L // 2) * freq_ids[None, :] % L
    angle = np.float32(2.0 * math.pi / L) * product.astype(np.float32)
    cos_table = np.cos(angle.astype(np.float64)).astype(ml_dtypes.bfloat16)
    sin_table = np.sin(angle.astype(np.float64)).astype(ml_dtypes.bfloat16)
    first = np.stack([cos_table, sin_table])
    second = np.concatenate(
        [
            np.concatenate([cos_table, -sin_table], axis=1),
            np.concatenate([-sin_table, -cos_table], axis=1),
        ],
        axis=0,
    ).astype(np.float32) / L
    return first, second.astype(ml_dtypes.bfloat16)


def transform(pictures, first, second):
    rows = jnp.einsum(
        "iyx,jkx->ijyk", pictures, jnp.asarray(first), preferred_element_type=jnp.float32
    ).astype(jnp.bfloat16)
    count_img = pictures.shape[0]
    rows = rows.reshape(count_img, 2 * L, L)
    parts = jnp.einsum(
        "ay,iyb->iab", jnp.asarray(second), rows, preferred_element_type=jnp.float32
    )
    parts = parts.reshape(count_img, 2, L, L // BLK, BLK)
    blocks = jnp.transpose(parts, (0, 2, 3, 1, 4))
    return blocks.reshape(count_img * PB, 2 * BLK).astype(jnp.bfloat16)


def ctf_rows(block_id, focus):
    row_id = block_id // (L // BLK)
    col_id = block_id % (L // BLK) * BLK
    lane_ids = jnp.arange(BLK, dtype=jnp.int32)
    freq_y = (row_id - L // 2).astype(jnp.float32) / L
    freq_x = (col_id[..., None] + lane_ids - L // 2).astype(jnp.float32) / L
    radius = freq_x * freq_x + (freq_y * freq_y)[..., None]
    return -jnp.sin(math.pi * focus.astype(jnp.float32)[..., None] * radius + phase_shift)


def residual_terms(prediction, observed, ctf_values, live_slots):
    shape = prediction.shape
    pred_wide = prediction.astype(jnp.float32).reshape(shape[:-1] + (2, BLK))
    obs_wide = observed.astype(jnp.float32).reshape(shape[:-1] + (2, BLK))
    factor = ctf_values[..., None, :]
    misfit = factor * (factor * pred_wide - obs_wide)
    misfit = jnp.where(live_slots[..., None, None], misfit, 0.0)
    return misfit.reshape(shape).astype(jnp.bfloat16)


def tap_matrix_t(tap_ids, weights, block_count):
    owners, taps, slots = tap_ids.shape
    flat_taps = jnp.transpose(tap_ids, (1, 0, 2)).reshape(taps, owners * slots)
    flat_weights = jnp.transpose(weights, (1, 0, 2)).reshape(taps, owners * slots)
    block_ids = jnp.arange(block_count, dtype=jnp.int32)
    picked = jnp.where(
        flat_taps[:, None, :] == block_ids[None, :, None],
        flat_weights[:, None, :],
        jnp.zeros((), jnp.bfloat16),
    )
    return jnp.sum(picked, axis=0, dtype=jnp.bfloat16)


def split_whole(values):
    return (values // 256).astype(jnp.bfloat16), (values % 256).astype(jnp.bfloat16)


def local(images, defocus, volume, counts, slot_pixel, slot_taps, slot_weights):
    first, second = dft_tables()
    extract = volume.astype(jnp.bfloat16)
    width = volume.shape[1]
    slot_count = counts[0, 0]
    pixel_ids = slot_pixel[0, 0]
    tap_ids = slot_taps[0, 0]
    weights = slot_weights[0, 0]
    owners, taps, capacity = tap_ids.shape
    live_slots = jnp.arange(capacity, dtype=jnp.int32)[None, :] < slot_count[:, None]
    tap_hi, tap_lo = split_whole(tap_ids)
    block_hi, block_lo = split_whole(pixel_ids % PB)
    pieces = [
        tap_hi,
        tap_lo,
        weights,
        block_hi[:, None, :],
        block_lo[:, None, :],
        defocus[pixel_ids // PB][:, None, :],
        live_slots.astype(jnp.bfloat16)[:, None, :],
    ]
    fields = sum(piece.shape[1] for piece in pieces)
    meta = jnp.zeros((owners, fields, capacity), jnp.bfloat16)
    offset = 0
    for piece in pieces:
        rows_of = piece.shape[1]
        meta = meta + jnp.pad(piece, ((0, 0), (offset, fields - offset - rows_of), (0, 0)))
        offset += rows_of
    got_meta = lax.all_to_all(meta, "vol", split_axis=0, concat_axis=0, tiled=True)
    observed = transform(images, first, second)
    flat_pixels = pixel_ids.reshape(-1)
    onehot = (flat_pixels[:, None] == jnp.arange(observed.shape[0], dtype=jnp.int32)[None, :])
    rows = jnp.dot(onehot.astype(jnp.bfloat16), observed, preferred_element_type=jnp.float32)
    rows = rows.astype(jnp.bfloat16).reshape(owners, capacity, width)
    got_rows = lax.all_to_all(rows, "vol", split_axis=0, concat_axis=0, tiled=True)
    whole = got_meta[:, : 2 * taps].astype(jnp.int32)
    got_taps = whole[:, :taps] * 256 + whole[:, taps:]
    got_weights = got_meta[:, 2 * taps : 3 * taps]
    block_parts = got_meta[:, 3 * taps : 3 * taps + 2].astype(jnp.int32)
    got_block = block_parts[:, 0] * 256 + block_parts[:, 1]
    got_focus = got_meta[:, 3 * taps + 2]
    got_live = got_meta[:, 3 * taps + 3] > 0.5
    matrix_t = tap_matrix_t(got_taps, got_weights, volume.shape[0])
    prediction = lax.dot_general(
        matrix_t, extract, (((0,), (0,)), ((), ())), preferred_element_type=jnp.float32
    )
    prediction = prediction.astype(jnp.bfloat16).reshape(owners, capacity, -1)
    ctf_values = ctf_rows(got_block, got_focus)
    weighted = residual_terms(prediction, got_rows, ctf_values, got_live)
    flat_residual = weighted.reshape(-1, width)
    gradient = jnp.dot(matrix_t, flat_residual, preferred_element_type=jnp.float32)
    shards = lax.axis_size("ptcl")
    if shards == 4:
        me = lax.axis_index("ptcl")
        on_chip = [(i, i ^ 1) for i in range(shards)]
        across = [(i, i ^ 2) for i in range(shards)]
        pair_sum = gradient + lax.ppermute(gradient, "ptcl", on_chip)
        half = gradient.shape[0] // 2
        core = me % 2
        mine = lax.dynamic_slice_in_dim(pair_sum, core * half, half, axis=0).astype(jnp.bfloat16)
        quarter = half // 2
        crossed = jnp.concatenate(
            [lax.ppermute(mine[:quarter], "ptcl", across), lax.ppermute(mine[quarter:], "ptcl", across)],
            axis=0,
        )
        total = mine.astype(jnp.float32) + crossed.astype(jnp.float32)
        updated = lax.dynamic_slice_in_dim(volume, core * half, half, axis=0) - learn_rate * total
        other = lax.ppermute(updated, "ptcl", on_chip)
        return jnp.where(
            core == 0,
            jnp.concatenate([updated, other], axis=0),
            jnp.concatenate([other, updated], axis=0),
        )
    partial = gradient.astype(jnp.bfloat16)
    parts = partial.reshape(shards, -1, gradient.shape[1])
    got_parts = lax.all_to_all(parts, "ptcl", split_axis=0, concat_axis=0, tiled=True)
    part_sum = jnp.sum(got_parts.astype(jnp.float32), axis=0)
    rows_each = part_sum.shape[0]
    start = lax.axis_index("ptcl") * rows_each
    mine = lax.dynamic_slice_in_dim(volume, start, rows_each, axis=0)
    updated = mine - learn_rate * part_sum
    return lax.all_gather(updated, "ptcl", axis=0, tiled=True)


def solution(mesh):
    placed = (
        P(("vol", "ptcl"), None, None),
        P(("vol", "ptcl")),
        P("vol", None),
        P("vol", "ptcl", None),
        P("vol", "ptcl", None, None),
        P("vol", "ptcl", None, None, None),
        P("vol", "ptcl", None, None, None),
    )
    return jax.shard_map(
        local, mesh=mesh, in_specs=placed, out_specs=P("vol", None), check_vma=False
    )
```

```python
import math

import jax
import jax.numpy as jnp
import ml_dtypes
import numpy as np
from jax import lax
from jax.experimental import pallas as pl
from jax.experimental.pallas import tpu as pltpu
from jax.sharding import PartitionSpec as P

L = 256
BLK = 128
PB = 512


learn_rate = 1.0
phase_shift = 0.1


def dft_tables():
    freq_ids = np.arange(L, dtype=np.int64)
    product = (freq_ids[:, None] - L // 2) * freq_ids[None, :] % L
    angle = np.float32(2.0 * math.pi / L) * product.astype(np.float32)
    cos_table = np.cos(angle.astype(np.float64)).astype(ml_dtypes.bfloat16)
    sin_table = np.sin(angle.astype(np.float64)).astype(ml_dtypes.bfloat16)
    first = np.stack([cos_table, sin_table])
    second = np.concatenate(
        [
            np.concatenate([cos_table, -sin_table], axis=1),
            np.concatenate([-sin_table, -cos_table], axis=1),
        ],
        axis=0,
    ).astype(np.float32) / L
    return first, second.astype(ml_dtypes.bfloat16)


def transform(pictures, first, second):
    rows = jnp.einsum(
        "iyx,jkx->ijyk", pictures, jnp.asarray(first), preferred_element_type=jnp.float32
    ).astype(jnp.bfloat16)
    count_img = pictures.shape[0]
    rows = rows.reshape(count_img, 2 * L, L)
    parts = jnp.einsum(
        "ay,iyb->iab", jnp.asarray(second), rows, preferred_element_type=jnp.float32
    )
    parts = parts.reshape(count_img, 2, L, L // BLK, BLK)
    blocks = jnp.transpose(parts, (0, 2, 3, 1, 4))
    return blocks.reshape(count_img * PB, 2 * BLK).astype(jnp.bfloat16)


def ctf_rows(block_id, focus):
    row_id = block_id // (L // BLK)
    col_id = block_id % (L // BLK) * BLK
    lane_ids = jnp.arange(BLK, dtype=jnp.int32)
    freq_y = (row_id - L // 2).astype(jnp.float32) / L
    freq_x = (col_id[..., None] + lane_ids - L // 2).astype(jnp.float32) / L
    radius = freq_x * freq_x + (freq_y * freq_y)[..., None]
    return -jnp.sin(math.pi * focus.astype(jnp.float32)[..., None] * radius + phase_shift)


def residual_terms(prediction, observed, ctf_values, live_slots):
    shape = prediction.shape
    pred_wide = prediction.astype(jnp.float32).reshape(shape[:-1] + (2, BLK))
    obs_wide = observed.astype(jnp.float32).reshape(shape[:-1] + (2, BLK))
    factor = ctf_values[..., None, :]
    misfit = factor * (factor * pred_wide - obs_wide)
    misfit = jnp.where(live_slots[..., None, None], misfit, 0.0)
    return misfit.reshape(shape).astype(jnp.bfloat16)


def tap_matrix_t(tap_ids, weights, block_count):
    owners, taps, slots = tap_ids.shape
    flat_taps = jnp.transpose(tap_ids, (1, 0, 2)).reshape(taps, owners * slots)
    flat_weights = jnp.transpose(weights, (1, 0, 2)).reshape(taps, owners * slots)
    block_ids = jnp.arange(block_count, dtype=jnp.int32)
    picked = jnp.where(
        flat_taps[:, None, :] == block_ids[None, :, None],
        flat_weights[:, None, :],
        jnp.zeros((), jnp.bfloat16),
    )
    return jnp.sum(picked, axis=0, dtype=jnp.bfloat16)


def split_whole(values):
    return (values // 256).astype(jnp.bfloat16), (values % 256).astype(jnp.bfloat16)


def meta_kernel(counts_ref, taps_ref, weights_ref, pixel_ref, focus_ref, out_ref):
    owners, taps, capacity = taps_ref.shape
    out_ref[:, 0:taps, :] = taps_ref[...].astype(jnp.float32)
    out_ref[:, taps : 2 * taps, :] = weights_ref[...].astype(jnp.float32)
    pixels = pixel_ref[...]
    image = pixels // PB
    focus_all = focus_ref[...].astype(jnp.float32)
    focus = jnp.zeros(pixels.shape, jnp.float32)
    for index in range(focus_all.shape[1]):
        focus = jnp.where(image == index, focus_all[:, index : index + 1], focus)
    block = (pixels % PB).astype(jnp.float32)
    lanes = lax.broadcasted_iota(jnp.int32, (1, capacity), 1)
    for owner in range(owners):
        out_ref[owner, 2 * taps : 2 * taps + 1, :] = block[owner : owner + 1]
        out_ref[owner, 2 * taps + 1 : 2 * taps + 2, :] = focus[owner : owner + 1]
        live = (lanes < counts_ref[owner]).astype(jnp.float32)
        out_ref[owner, 2 * taps + 2 : 2 * taps + 3, :] = live


def slot_meta(counts, tap_ids, weights, pixel_ids, defocus):
    owners, taps, capacity = tap_ids.shape
    vmem = pltpu.MemorySpace.VMEM
    return pl.pallas_call(
        meta_kernel,
        out_shape=jax.ShapeDtypeStruct((owners, 2 * taps + 3, capacity), jnp.float32),
        in_specs=[
            pl.BlockSpec(memory_space=pltpu.MemorySpace.SMEM),
            pl.BlockSpec(memory_space=vmem),
            pl.BlockSpec(memory_space=vmem),
            pl.BlockSpec(memory_space=vmem),
            pl.BlockSpec(memory_space=vmem),
        ],
        out_specs=pl.BlockSpec(memory_space=vmem),
    )(counts, tap_ids, weights, pixel_ids, defocus.reshape(1, -1))


def local(images, defocus, volume, counts, slot_pixel, slot_taps, slot_weights):
    first, second = dft_tables()
    extract = volume.astype(jnp.bfloat16)
    width = volume.shape[1]
    slot_count = counts[0, 0]
    pixel_ids = slot_pixel[0, 0]
    tap_ids = slot_taps[0, 0]
    weights = slot_weights[0, 0]
    owners, taps, capacity = tap_ids.shape
    meta = slot_meta(slot_count, tap_ids, weights, pixel_ids, defocus)
    got_meta = lax.all_to_all(meta, "vol", split_axis=0, concat_axis=0, tiled=True)
    observed = transform(images, first, second)
    flat_pixels = pixel_ids.reshape(-1)
    onehot = (flat_pixels[:, None] == jnp.arange(observed.shape[0], dtype=jnp.int32)[None, :])
    rows = jnp.dot(onehot.astype(jnp.bfloat16), observed, preferred_element_type=jnp.float32)
    rows = rows.astype(jnp.bfloat16).reshape(owners, capacity, width)
    got_rows = lax.all_to_all(rows, "vol", split_axis=0, concat_axis=0, tiled=True)
    got_taps = got_meta[:, :taps].astype(jnp.int32)
    got_weights = got_meta[:, taps : 2 * taps].astype(jnp.bfloat16)
    got_block = got_meta[:, 2 * taps].astype(jnp.int32)
    got_focus = got_meta[:, 2 * taps + 1]
    got_live = got_meta[:, 2 * taps + 2] > 0.5
    matrix_t = tap_matrix_t(got_taps, got_weights, volume.shape[0])
    prediction = lax.dot_general(
        matrix_t, extract, (((0,), (0,)), ((), ())), preferred_element_type=jnp.float32
    )
    prediction = prediction.astype(jnp.bfloat16).reshape(owners, capacity, -1)
    ctf_values = ctf_rows(got_block, got_focus)
    weighted = residual_terms(prediction, got_rows, ctf_values, got_live)
    flat_residual = weighted.reshape(-1, width)
    gradient = jnp.dot(matrix_t, flat_residual, preferred_element_type=jnp.float32)
    shards = lax.axis_size("ptcl")
    if shards == 4:
        me = lax.axis_index("ptcl")
        on_chip = [(i, i ^ 1) for i in range(shards)]
        across = [(i, i ^ 2) for i in range(shards)]
        pair_sum = gradient + lax.ppermute(gradient, "ptcl", on_chip)
        half = gradient.shape[0] // 2
        core = me % 2
        mine = lax.dynamic_slice_in_dim(pair_sum, core * half, half, axis=0).astype(jnp.bfloat16)
        total = mine.astype(jnp.float32) + lax.ppermute(mine, "ptcl", across).astype(jnp.float32)
        updated = lax.dynamic_slice_in_dim(volume, core * half, half, axis=0) - learn_rate * total
        other = lax.ppermute(updated, "ptcl", on_chip)
        return jnp.where(
            core == 0,
            jnp.concatenate([updated, other], axis=0),
            jnp.concatenate([other, updated], axis=0),
        )
    partial = gradient.astype(jnp.bfloat16)
    parts = partial.reshape(shards, -1, gradient.shape[1])
    got_parts = lax.all_to_all(parts, "ptcl", split_axis=0, concat_axis=0, tiled=True)
    part_sum = jnp.sum(got_parts.astype(jnp.float32), axis=0)
    rows_each = part_sum.shape[0]
    start = lax.axis_index("ptcl") * rows_each
    mine = lax.dynamic_slice_in_dim(volume, start, rows_each, axis=0)
    updated = mine - learn_rate * part_sum
    return lax.all_gather(updated, "ptcl", axis=0, tiled=True)


def solution(mesh):
    placed = (
        P(("vol", "ptcl"), None, None),
        P(("vol", "ptcl")),
        P("vol", None),
        P("vol", "ptcl", None),
        P("vol", "ptcl", None, None),
        P("vol", "ptcl", None, None, None),
        P("vol", "ptcl", None, None, None),
    )
    return jax.shard_map(
        local, mesh=mesh, in_specs=placed, out_specs=P("vol", None), check_vma=False
    )
```

```python
import math

import jax
import jax.numpy as jnp
import ml_dtypes
import numpy as np
from jax import lax
from jax.experimental import pallas as pl
from jax.experimental.pallas import tpu as pltpu
from jax.sharding import PartitionSpec as P

L = 256
BLK = 128
PB = 512


learn_rate = 1.0
phase_shift = 0.1


def dft_tables():
    freq_ids = np.arange(L, dtype=np.int64)
    product = (freq_ids[:, None] - L // 2) * freq_ids[None, :] % L
    angle = np.float32(2.0 * math.pi / L) * product.astype(np.float32)
    cos_table = np.cos(angle.astype(np.float64)).astype(ml_dtypes.bfloat16)
    sin_table = np.sin(angle.astype(np.float64)).astype(ml_dtypes.bfloat16)
    first = np.stack([cos_table, sin_table])
    second = np.concatenate(
        [
            np.concatenate([cos_table, -sin_table], axis=1),
            np.concatenate([-sin_table, -cos_table], axis=1),
        ],
        axis=0,
    ).astype(np.float32) / L
    return first, second.astype(ml_dtypes.bfloat16)


def transform(pictures, first, second):
    rows = jnp.einsum(
        "iyx,jkx->ijyk", pictures, jnp.asarray(first), preferred_element_type=jnp.float32
    ).astype(jnp.bfloat16)
    count_img = pictures.shape[0]
    rows = rows.reshape(count_img, 2 * L, L)
    parts = jnp.einsum(
        "ay,iyb->iab", jnp.asarray(second), rows, preferred_element_type=jnp.float32
    )
    parts = parts.reshape(count_img, 2, L, L // BLK, BLK)
    blocks = jnp.transpose(parts, (0, 2, 3, 1, 4))
    return blocks.reshape(count_img * PB, 2 * BLK).astype(jnp.bfloat16)


def ctf_rows(block_id, focus):
    row_id = block_id // (L // BLK)
    col_id = block_id % (L // BLK) * BLK
    lane_ids = jnp.arange(BLK, dtype=jnp.int32)
    freq_y = (row_id - L // 2).astype(jnp.float32) / L
    freq_x = (col_id[..., None] + lane_ids - L // 2).astype(jnp.float32) / L
    radius = freq_x * freq_x + (freq_y * freq_y)[..., None]
    return -jnp.sin(math.pi * focus.astype(jnp.float32)[..., None] * radius + phase_shift)


def residual_terms(prediction, observed, ctf_values, live_slots):
    shape = prediction.shape
    pred_wide = prediction.astype(jnp.float32).reshape(shape[:-1] + (2, BLK))
    obs_wide = observed.astype(jnp.float32).reshape(shape[:-1] + (2, BLK))
    factor = ctf_values[..., None, :]
    misfit = factor * (factor * pred_wide - obs_wide)
    misfit = jnp.where(live_slots[..., None, None], misfit, 0.0)
    return misfit.reshape(shape).astype(jnp.bfloat16)


def tap_matrix_t(tap_ids, weights, block_count):
    owners, taps, slots = tap_ids.shape
    flat_taps = jnp.transpose(tap_ids, (1, 0, 2)).reshape(taps, owners * slots)
    flat_weights = jnp.transpose(weights, (1, 0, 2)).reshape(taps, owners * slots)
    block_ids = jnp.arange(block_count, dtype=jnp.int32)
    picked = jnp.where(
        flat_taps[:, None, :] == block_ids[None, :, None],
        flat_weights[:, None, :],
        jnp.zeros((), jnp.bfloat16),
    )
    return jnp.sum(picked, axis=0, dtype=jnp.bfloat16)


def split_whole(values):
    return (values // 256).astype(jnp.bfloat16), (values % 256).astype(jnp.bfloat16)


def meta_kernel(counts_ref, taps_ref, weights_ref, pixel_ref, focus_ref, out_ref):
    owners, taps, capacity = taps_ref.shape
    out_ref[:, 0:taps, :] = taps_ref[...].astype(jnp.float32)
    out_ref[:, taps : 2 * taps, :] = weights_ref[...].astype(jnp.float32)
    pixels = pixel_ref[...]
    image = pixels // PB
    focus_all = focus_ref[...].astype(jnp.float32)
    focus = jnp.zeros(pixels.shape, jnp.float32)
    for index in range(focus_all.shape[1]):
        focus = jnp.where(image == index, focus_all[:, index : index + 1], focus)
    block = (pixels % PB).astype(jnp.float32)
    lanes = lax.broadcasted_iota(jnp.int32, (1, capacity), 1)
    for owner in range(owners):
        out_ref[owner, 2 * taps : 2 * taps + 1, :] = block[owner : owner + 1]
        out_ref[owner, 2 * taps + 1 : 2 * taps + 2, :] = focus[owner : owner + 1]
        live = (lanes < counts_ref[owner]).astype(jnp.float32)
        out_ref[owner, 2 * taps + 2 : 2 * taps + 3, :] = live


def slot_meta(counts, tap_ids, weights, pixel_ids, defocus):
    owners, taps, capacity = tap_ids.shape
    vmem = pltpu.MemorySpace.VMEM
    return pl.pallas_call(
        meta_kernel,
        out_shape=jax.ShapeDtypeStruct((owners, 2 * taps + 3, capacity), jnp.float32),
        in_specs=[
            pl.BlockSpec(memory_space=pltpu.MemorySpace.SMEM),
            pl.BlockSpec(memory_space=vmem),
            pl.BlockSpec(memory_space=vmem),
            pl.BlockSpec(memory_space=vmem),
            pl.BlockSpec(memory_space=vmem),
        ],
        out_specs=pl.BlockSpec(memory_space=vmem),
    )(counts, tap_ids, weights, pixel_ids, defocus.reshape(1, -1))


def local(images, defocus, volume, counts, slot_pixel, slot_taps, slot_weights):
    first, second = dft_tables()
    extract = volume.astype(jnp.bfloat16)
    width = volume.shape[1]
    slot_count = counts[0, 0]
    pixel_ids = slot_pixel[0, 0]
    tap_ids = slot_taps[0, 0]
    weights = slot_weights[0, 0]
    owners, taps, capacity = tap_ids.shape
    meta = slot_meta(slot_count, tap_ids, weights, pixel_ids, defocus)
    observed = transform(images, first, second)
    flat_pixels = pixel_ids.reshape(-1)
    onehot = (flat_pixels[:, None] == jnp.arange(observed.shape[0], dtype=jnp.int32)[None, :])
    rows = jnp.dot(onehot.astype(jnp.bfloat16), observed, preferred_element_type=jnp.float32)
    rows = rows.astype(jnp.bfloat16).reshape(owners, capacity, width)
    meta, rows = lax.optimization_barrier((meta, rows))
    got_meta = lax.all_to_all(meta, "vol", split_axis=0, concat_axis=0, tiled=True)
    got_rows = lax.all_to_all(rows, "vol", split_axis=0, concat_axis=0, tiled=True)
    got_taps = got_meta[:, :taps].astype(jnp.int32)
    got_weights = got_meta[:, taps : 2 * taps].astype(jnp.bfloat16)
    got_block = got_meta[:, 2 * taps].astype(jnp.int32)
    got_focus = got_meta[:, 2 * taps + 1]
    got_live = got_meta[:, 2 * taps + 2] > 0.5
    matrix_t = tap_matrix_t(got_taps, got_weights, volume.shape[0])
    prediction = lax.dot_general(
        matrix_t, extract, (((0,), (0,)), ((), ())), preferred_element_type=jnp.float32
    )
    prediction = prediction.astype(jnp.bfloat16).reshape(owners, capacity, -1)
    ctf_values = ctf_rows(got_block, got_focus)
    weighted = residual_terms(prediction, got_rows, ctf_values, got_live)
    flat_residual = weighted.reshape(-1, width)
    gradient = jnp.dot(matrix_t, flat_residual, preferred_element_type=jnp.float32)
    shards = lax.axis_size("ptcl")
    if shards == 4:
        me = lax.axis_index("ptcl")
        on_chip = [(i, i ^ 1) for i in range(shards)]
        across = [(i, i ^ 2) for i in range(shards)]
        pair_sum = gradient + lax.ppermute(gradient, "ptcl", on_chip)
        half = gradient.shape[0] // 2
        core = me % 2
        mine = lax.dynamic_slice_in_dim(pair_sum, core * half, half, axis=0).astype(jnp.bfloat16)
        total = mine.astype(jnp.float32) + lax.ppermute(mine, "ptcl", across).astype(jnp.float32)
        updated = lax.dynamic_slice_in_dim(volume, core * half, half, axis=0) - learn_rate * total
        other = lax.ppermute(updated, "ptcl", on_chip)
        return jnp.where(
            core == 0,
            jnp.concatenate([updated, other], axis=0),
            jnp.concatenate([other, updated], axis=0),
        )
    partial = gradient.astype(jnp.bfloat16)
    parts = partial.reshape(shards, -1, gradient.shape[1])
    got_parts = lax.all_to_all(parts, "ptcl", split_axis=0, concat_axis=0, tiled=True)
    part_sum = jnp.sum(got_parts.astype(jnp.float32), axis=0)
    rows_each = part_sum.shape[0]
    start = lax.axis_index("ptcl") * rows_each
    mine = lax.dynamic_slice_in_dim(volume, start, rows_each, axis=0)
    updated = mine - learn_rate * part_sum
    return lax.all_gather(updated, "ptcl", axis=0, tiled=True)


def solution(mesh):
    placed = (
        P(("vol", "ptcl"), None, None),
        P(("vol", "ptcl")),
        P("vol", None),
        P("vol", "ptcl", None),
        P("vol", "ptcl", None, None),
        P("vol", "ptcl", None, None, None),
        P("vol", "ptcl", None, None, None),
    )
    return jax.shard_map(
        local, mesh=mesh, in_specs=placed, out_specs=P("vol", None), check_vma=False
    )
```

```python
import math

import jax
import jax.numpy as jnp
import ml_dtypes
import numpy as np
from jax import lax
from jax.experimental import pallas as pl
from jax.experimental.pallas import tpu as pltpu
from jax.sharding import PartitionSpec as P

L = 256
BLK = 128
PB = 512


learn_rate = 1.0
phase_shift = 0.1


def dft_tables():
    freq_ids = np.arange(L, dtype=np.int64)
    product = (freq_ids[:, None] - L // 2) * freq_ids[None, :] % L
    angle = np.float32(2.0 * math.pi / L) * product.astype(np.float32)
    cos_table = np.cos(angle.astype(np.float64)).astype(ml_dtypes.bfloat16)
    sin_table = np.sin(angle.astype(np.float64)).astype(ml_dtypes.bfloat16)
    first = np.stack([cos_table, sin_table])
    second = np.concatenate(
        [
            np.concatenate([cos_table, -sin_table], axis=1),
            np.concatenate([-sin_table, -cos_table], axis=1),
        ],
        axis=0,
    ).astype(np.float32) / L
    return first, second.astype(ml_dtypes.bfloat16)


def transform(pictures, first, second):
    rows = jnp.einsum(
        "iyx,jkx->ijyk", pictures, jnp.asarray(first), preferred_element_type=jnp.float32
    ).astype(jnp.bfloat16)
    count_img = pictures.shape[0]
    rows = rows.reshape(count_img, 2 * L, L)
    parts = jnp.einsum(
        "ay,iyb->iab", jnp.asarray(second), rows, preferred_element_type=jnp.float32
    )
    parts = parts.reshape(count_img, 2, L, L // BLK, BLK)
    blocks = jnp.transpose(parts, (0, 2, 3, 1, 4))
    return blocks.reshape(count_img * PB, 2 * BLK).astype(jnp.bfloat16)


def ctf_rows(block_id, focus):
    row_id = block_id // (L // BLK)
    col_id = block_id % (L // BLK) * BLK
    lane_ids = jnp.arange(BLK, dtype=jnp.int32)
    freq_y = (row_id - L // 2).astype(jnp.float32) / L
    freq_x = (col_id[..., None] + lane_ids - L // 2).astype(jnp.float32) / L
    radius = freq_x * freq_x + (freq_y * freq_y)[..., None]
    return -jnp.sin(math.pi * focus.astype(jnp.float32)[..., None] * radius + phase_shift)


def residual_terms(prediction, observed, ctf_values, live_slots):
    shape = prediction.shape
    pred_wide = prediction.astype(jnp.float32).reshape(shape[:-1] + (2, BLK))
    obs_wide = observed.astype(jnp.float32).reshape(shape[:-1] + (2, BLK))
    factor = ctf_values[..., None, :]
    misfit = factor * (factor * pred_wide - obs_wide)
    misfit = jnp.where(live_slots[..., None, None], misfit, 0.0)
    return misfit.reshape(shape).astype(jnp.bfloat16)


def tap_matrix_t(tap_ids, weights, block_count):
    owners, taps, slots = tap_ids.shape
    flat_taps = jnp.transpose(tap_ids, (1, 0, 2)).reshape(taps, owners * slots)
    flat_weights = jnp.transpose(weights, (1, 0, 2)).reshape(taps, owners * slots)
    block_ids = jnp.arange(block_count, dtype=jnp.int32)
    picked = jnp.where(
        flat_taps[:, None, :] == block_ids[None, :, None],
        flat_weights[:, None, :],
        jnp.zeros((), jnp.bfloat16),
    )
    return jnp.sum(picked, axis=0, dtype=jnp.bfloat16)


def split_whole(values):
    return (values // 256).astype(jnp.bfloat16), (values % 256).astype(jnp.bfloat16)


def meta_kernel(counts_ref, taps_ref, weights_ref, pixel_ref, focus_ref, out_ref):
    owners, taps, capacity = taps_ref.shape
    out_ref[:, 0:taps, :] = taps_ref[...].astype(jnp.float32)
    out_ref[:, taps : 2 * taps, :] = weights_ref[...].astype(jnp.float32)
    pixels = pixel_ref[...]
    image = pixels // PB
    focus_all = focus_ref[...].astype(jnp.float32)
    focus = jnp.zeros(pixels.shape, jnp.float32)
    for index in range(focus_all.shape[1]):
        focus = jnp.where(image == index, focus_all[:, index : index + 1], focus)
    block = (pixels % PB).astype(jnp.float32)
    lanes = lax.broadcasted_iota(jnp.int32, (1, capacity), 1)
    for owner in range(owners):
        out_ref[owner, 2 * taps : 2 * taps + 1, :] = block[owner : owner + 1]
        out_ref[owner, 2 * taps + 1 : 2 * taps + 2, :] = focus[owner : owner + 1]
        live = (lanes < counts_ref[owner]).astype(jnp.float32)
        out_ref[owner, 2 * taps + 2 : 2 * taps + 3, :] = live


def slot_meta(counts, tap_ids, weights, pixel_ids, defocus):
    owners, taps, capacity = tap_ids.shape
    vmem = pltpu.MemorySpace.VMEM
    return pl.pallas_call(
        meta_kernel,
        out_shape=jax.ShapeDtypeStruct((owners, 2 * taps + 3, capacity), jnp.float32),
        in_specs=[
            pl.BlockSpec(memory_space=pltpu.MemorySpace.SMEM),
            pl.BlockSpec(memory_space=vmem),
            pl.BlockSpec(memory_space=vmem),
            pl.BlockSpec(memory_space=vmem),
            pl.BlockSpec(memory_space=vmem),
        ],
        out_specs=pl.BlockSpec(memory_space=vmem),
    )(counts, tap_ids, weights, pixel_ids, defocus.reshape(1, -1))


def local(images, defocus, volume, counts, slot_pixel, slot_taps, slot_weights):
    first, second = dft_tables()
    extract = volume.astype(jnp.bfloat16)
    width = volume.shape[1]
    slot_count = counts[0, 0]
    pixel_ids = slot_pixel[0, 0]
    tap_ids = slot_taps[0, 0]
    weights = slot_weights[0, 0]
    owners, taps, capacity = tap_ids.shape
    meta = slot_meta(slot_count, tap_ids, weights, pixel_ids, defocus)
    got_meta = lax.all_to_all(meta, "vol", split_axis=0, concat_axis=0, tiled=True)
    observed = transform(images, first, second)
    flat_pixels = pixel_ids.reshape(-1)
    onehot = (flat_pixels[:, None] == jnp.arange(observed.shape[0], dtype=jnp.int32)[None, :])
    rows = jnp.dot(onehot.astype(jnp.bfloat16), observed, preferred_element_type=jnp.float32)
    rows = rows.astype(jnp.bfloat16).reshape(owners, capacity, width)
    got_rows = lax.all_to_all(rows, "vol", split_axis=0, concat_axis=0, tiled=True)
    got_taps = got_meta[:, :taps].astype(jnp.int32)
    got_weights = got_meta[:, taps : 2 * taps].astype(jnp.bfloat16)
    got_block = got_meta[:, 2 * taps].astype(jnp.int32)
    got_focus = got_meta[:, 2 * taps + 1]
    got_live = got_meta[:, 2 * taps + 2] > 0.5
    matrix_t = tap_matrix_t(got_taps, got_weights, volume.shape[0])
    prediction = lax.dot_general(
        matrix_t, extract, (((0,), (0,)), ((), ())), preferred_element_type=jnp.float32
    )
    prediction = prediction.astype(jnp.bfloat16).reshape(owners, capacity, -1)
    ctf_values = ctf_rows(got_block, got_focus)
    weighted = residual_terms(prediction, got_rows, ctf_values, got_live)
    flat_residual = weighted.reshape(-1, width)
    shards = lax.axis_size("ptcl")
    if shards == 4:
        me = lax.axis_index("ptcl")
        on_chip = [(i, i ^ 1) for i in range(shards)]
        across = [(i, i ^ 2) for i in range(shards)]
        half = matrix_t.shape[0] // 2
        core = me % 2
        for_sibling = jnp.dot(
            lax.dynamic_slice_in_dim(matrix_t, (1 - core) * half, half, axis=0),
            flat_residual,
            preferred_element_type=jnp.float32,
        )
        arrived = lax.ppermute(for_sibling, "ptcl", on_chip)
        own = jnp.dot(
            lax.dynamic_slice_in_dim(matrix_t, core * half, half, axis=0),
            flat_residual,
            preferred_element_type=jnp.float32,
        )
        mine = (own + arrived).astype(jnp.bfloat16)
        total = mine.astype(jnp.float32) + lax.ppermute(mine, "ptcl", across).astype(jnp.float32)
        updated = lax.dynamic_slice_in_dim(volume, core * half, half, axis=0) - learn_rate * total
        other = lax.ppermute(updated, "ptcl", on_chip)
        return jnp.where(
            core == 0,
            jnp.concatenate([updated, other], axis=0),
            jnp.concatenate([other, updated], axis=0),
        )
    gradient = jnp.dot(matrix_t, flat_residual, preferred_element_type=jnp.float32)
    partial = gradient.astype(jnp.bfloat16)
    parts = partial.reshape(shards, -1, gradient.shape[1])
    got_parts = lax.all_to_all(parts, "ptcl", split_axis=0, concat_axis=0, tiled=True)
    part_sum = jnp.sum(got_parts.astype(jnp.float32), axis=0)
    rows_each = part_sum.shape[0]
    start = lax.axis_index("ptcl") * rows_each
    mine = lax.dynamic_slice_in_dim(volume, start, rows_each, axis=0)
    updated = mine - learn_rate * part_sum
    return lax.all_gather(updated, "ptcl", axis=0, tiled=True)


def solution(mesh):
    placed = (
        P(("vol", "ptcl"), None, None),
        P(("vol", "ptcl")),
        P("vol", None),
        P("vol", "ptcl", None),
        P("vol", "ptcl", None, None),
        P("vol", "ptcl", None, None, None),
        P("vol", "ptcl", None, None, None),
    )
    return jax.shard_map(
        local, mesh=mesh, in_specs=placed, out_specs=P("vol", None), check_vma=False
    )
```

```python
import math

import jax
import jax.numpy as jnp
import ml_dtypes
import numpy as np
from jax import lax
from jax.experimental import pallas as pl
from jax.experimental.pallas import tpu as pltpu
from jax.sharding import PartitionSpec as P

L = 256
BLK = 128
PB = 512


learn_rate = 1.0
phase_shift = 0.1


def dft_tables():
    freq_ids = np.arange(L, dtype=np.int64)
    product = (freq_ids[:, None] - L // 2) * freq_ids[None, :] % L
    angle = np.float32(2.0 * math.pi / L) * product.astype(np.float32)
    cos_table = np.cos(angle.astype(np.float64)).astype(ml_dtypes.bfloat16)
    sin_table = np.sin(angle.astype(np.float64)).astype(ml_dtypes.bfloat16)
    first = np.stack([cos_table, sin_table])
    second = np.concatenate(
        [
            np.concatenate([cos_table, -sin_table], axis=1),
            np.concatenate([-sin_table, -cos_table], axis=1),
        ],
        axis=0,
    ).astype(np.float32) / L
    return first, second.astype(ml_dtypes.bfloat16)


def transform(pictures, first, second):
    rows = jnp.einsum(
        "iyx,jkx->ijyk", pictures, jnp.asarray(first), preferred_element_type=jnp.float32
    ).astype(jnp.bfloat16)
    count_img = pictures.shape[0]
    rows = rows.reshape(count_img, 2 * L, L)
    parts = jnp.einsum(
        "ay,iyb->iab", jnp.asarray(second), rows, preferred_element_type=jnp.float32
    )
    parts = parts.reshape(count_img, 2, L, L // BLK, BLK)
    blocks = jnp.transpose(parts, (0, 2, 3, 1, 4))
    return blocks.reshape(count_img * PB, 2 * BLK).astype(jnp.bfloat16)


def ctf_rows(block_id, focus):
    row_id = block_id // (L // BLK)
    col_id = block_id % (L // BLK) * BLK
    lane_ids = jnp.arange(BLK, dtype=jnp.int32)
    freq_y = (row_id - L // 2).astype(jnp.float32) / L
    freq_x = (col_id[..., None] + lane_ids - L // 2).astype(jnp.float32) / L
    radius = freq_x * freq_x + (freq_y * freq_y)[..., None]
    return -jnp.sin(math.pi * focus.astype(jnp.float32)[..., None] * radius + phase_shift)


def residual_terms(prediction, observed, ctf_values, live_slots):
    shape = prediction.shape
    pred_wide = prediction.astype(jnp.float32).reshape(shape[:-1] + (2, BLK))
    obs_wide = observed.astype(jnp.float32).reshape(shape[:-1] + (2, BLK))
    factor = ctf_values[..., None, :]
    misfit = factor * (factor * pred_wide - obs_wide)
    misfit = jnp.where(live_slots[..., None, None], misfit, 0.0)
    return misfit.reshape(shape).astype(jnp.bfloat16)


def tap_matrix_t(tap_ids, weights, block_count):
    owners, taps, slots = tap_ids.shape
    flat_taps = jnp.transpose(tap_ids, (1, 0, 2)).reshape(taps, owners * slots)
    flat_weights = jnp.transpose(weights, (1, 0, 2)).reshape(taps, owners * slots)
    block_ids = jnp.arange(block_count, dtype=jnp.int32)
    picked = jnp.where(
        flat_taps[:, None, :] == block_ids[None, :, None],
        flat_weights[:, None, :],
        jnp.zeros((), jnp.bfloat16),
    )
    return jnp.sum(picked, axis=0, dtype=jnp.bfloat16)


def split_whole(values):
    return (values // 256).astype(jnp.bfloat16), (values % 256).astype(jnp.bfloat16)


def meta_kernel(counts_ref, taps_ref, weights_ref, pixel_ref, focus_ref, out_ref):
    owners, taps, capacity = taps_ref.shape
    out_ref[:, 0:taps, :] = taps_ref[...].astype(jnp.float32)
    out_ref[:, taps : 2 * taps, :] = weights_ref[...].astype(jnp.float32)
    pixels = pixel_ref[...]
    image = pixels // PB
    focus_all = focus_ref[...].astype(jnp.float32)
    focus = jnp.zeros(pixels.shape, jnp.float32)
    for index in range(focus_all.shape[1]):
        focus = jnp.where(image == index, focus_all[:, index : index + 1], focus)
    block = (pixels % PB).astype(jnp.float32)
    lanes = lax.broadcasted_iota(jnp.int32, (1, capacity), 1)
    for owner in range(owners):
        out_ref[owner, 2 * taps : 2 * taps + 1, :] = block[owner : owner + 1]
        out_ref[owner, 2 * taps + 1 : 2 * taps + 2, :] = focus[owner : owner + 1]
        live = (lanes < counts_ref[owner]).astype(jnp.float32)
        out_ref[owner, 2 * taps + 2 : 2 * taps + 3, :] = live


def slot_meta(counts, tap_ids, weights, pixel_ids, defocus):
    owners, taps, capacity = tap_ids.shape
    vmem = pltpu.MemorySpace.VMEM
    return pl.pallas_call(
        meta_kernel,
        out_shape=jax.ShapeDtypeStruct((owners, 2 * taps + 3, capacity), jnp.float32),
        in_specs=[
            pl.BlockSpec(memory_space=pltpu.MemorySpace.SMEM),
            pl.BlockSpec(memory_space=vmem),
            pl.BlockSpec(memory_space=vmem),
            pl.BlockSpec(memory_space=vmem),
            pl.BlockSpec(memory_space=vmem),
        ],
        out_specs=pl.BlockSpec(memory_space=vmem),
    )(counts, tap_ids, weights, pixel_ids, defocus.reshape(1, -1))


def local(images, defocus, volume, counts, slot_pixel, slot_taps, slot_weights):
    first, second = dft_tables()
    extract = volume.astype(jnp.bfloat16)
    width = volume.shape[1]
    slot_count = counts[0, 0]
    pixel_ids = slot_pixel[0, 0]
    tap_ids = slot_taps[0, 0]
    weights = slot_weights[0, 0]
    owners, taps, capacity = tap_ids.shape
    warm = lax.ppermute(slot_count[:1].astype(jnp.float32), "vol",
                        [(i, (i + 1) % lax.axis_size("vol")) for i in range(lax.axis_size("vol"))])
    meta = slot_meta(slot_count, tap_ids, weights, pixel_ids, defocus)
    meta, warm = lax.optimization_barrier((meta, warm))
    got_meta = lax.all_to_all(meta, "vol", split_axis=0, concat_axis=0, tiled=True)
    observed = transform(images, first, second)
    flat_pixels = pixel_ids.reshape(-1)
    onehot = (flat_pixels[:, None] == jnp.arange(observed.shape[0], dtype=jnp.int32)[None, :])
    rows = jnp.dot(onehot.astype(jnp.bfloat16), observed, preferred_element_type=jnp.float32)
    rows = rows.astype(jnp.bfloat16).reshape(owners, capacity, width)
    got_rows = lax.all_to_all(rows, "vol", split_axis=0, concat_axis=0, tiled=True)
    got_taps = got_meta[:, :taps].astype(jnp.int32)
    got_weights = got_meta[:, taps : 2 * taps].astype(jnp.bfloat16)
    got_block = got_meta[:, 2 * taps].astype(jnp.int32)
    got_focus = got_meta[:, 2 * taps + 1]
    got_live = got_meta[:, 2 * taps + 2] > 0.5
    matrix_t = tap_matrix_t(got_taps, got_weights, volume.shape[0])
    prediction = lax.dot_general(
        matrix_t, extract, (((0,), (0,)), ((), ())), preferred_element_type=jnp.float32
    )
    prediction = prediction.astype(jnp.bfloat16).reshape(owners, capacity, -1)
    ctf_values = ctf_rows(got_block, got_focus)
    weighted = residual_terms(prediction, got_rows, ctf_values, got_live)
    flat_residual = weighted.reshape(-1, width)
    shards = lax.axis_size("ptcl")
    if shards == 4:
        me = lax.axis_index("ptcl")
        on_chip = [(i, i ^ 1) for i in range(shards)]
        across = [(i, i ^ 2) for i in range(shards)]
        half = matrix_t.shape[0] // 2
        core = me % 2
        for_sibling = jnp.dot(
            lax.dynamic_slice_in_dim(matrix_t, (1 - core) * half, half, axis=0),
            flat_residual,
            preferred_element_type=jnp.float32,
        )
        arrived = lax.ppermute(for_sibling, "ptcl", on_chip)
        own = jnp.dot(
            lax.dynamic_slice_in_dim(matrix_t, core * half, half, axis=0),
            flat_residual,
            preferred_element_type=jnp.float32,
        )
        mine = (own + arrived).astype(jnp.bfloat16)
        total = mine.astype(jnp.float32) + lax.ppermute(mine, "ptcl", across).astype(jnp.float32)
        updated = lax.dynamic_slice_in_dim(volume, core * half, half, axis=0) - learn_rate * total
        other = lax.ppermute(updated, "ptcl", on_chip)
        zero = warm[0] * 0.0
        return zero + jnp.where(
            core == 0,
            jnp.concatenate([updated, other], axis=0),
            jnp.concatenate([other, updated], axis=0),
        )
    gradient = jnp.dot(matrix_t, flat_residual, preferred_element_type=jnp.float32)
    partial = gradient.astype(jnp.bfloat16)
    parts = partial.reshape(shards, -1, gradient.shape[1])
    got_parts = lax.all_to_all(parts, "ptcl", split_axis=0, concat_axis=0, tiled=True)
    part_sum = jnp.sum(got_parts.astype(jnp.float32), axis=0)
    rows_each = part_sum.shape[0]
    start = lax.axis_index("ptcl") * rows_each
    mine = lax.dynamic_slice_in_dim(volume, start, rows_each, axis=0)
    updated = mine - learn_rate * part_sum
    return lax.all_gather(updated, "ptcl", axis=0, tiled=True)


def solution(mesh):
    placed = (
        P(("vol", "ptcl"), None, None),
        P(("vol", "ptcl")),
        P("vol", None),
        P("vol", "ptcl", None),
        P("vol", "ptcl", None, None),
        P("vol", "ptcl", None, None, None),
        P("vol", "ptcl", None, None, None),
    )
    return jax.shard_map(
        local, mesh=mesh, in_specs=placed, out_specs=P("vol", None), check_vma=False
    )
```

```python
import math

import jax
import jax.numpy as jnp
import ml_dtypes
import numpy as np
from jax import lax
from jax.experimental import pallas as pl
from jax.experimental.pallas import tpu as pltpu
from jax.sharding import PartitionSpec as P

L = 256
BLK = 128
PB = 512


learn_rate = 1.0
phase_shift = 0.1


def dft_tables():
    freq_ids = np.arange(L, dtype=np.int64)
    product = (freq_ids[:, None] - L // 2) * freq_ids[None, :] % L
    angle = np.float32(2.0 * math.pi / L) * product.astype(np.float32)
    cos_table = np.cos(angle.astype(np.float64)).astype(ml_dtypes.bfloat16)
    sin_table = np.sin(angle.astype(np.float64)).astype(ml_dtypes.bfloat16)
    first = np.stack([cos_table, sin_table])
    second = np.concatenate(
        [
            np.concatenate([cos_table, -sin_table], axis=1),
            np.concatenate([-sin_table, -cos_table], axis=1),
        ],
        axis=0,
    ).astype(np.float32) / L
    return first, second.astype(ml_dtypes.bfloat16)


def transform(pictures, first, second):
    rows = jnp.einsum(
        "iyx,jkx->ijyk", pictures, jnp.asarray(first), preferred_element_type=jnp.float32
    ).astype(jnp.bfloat16)
    count_img = pictures.shape[0]
    rows = rows.reshape(count_img, 2 * L, L)
    parts = jnp.einsum(
        "ay,iyb->iab", jnp.asarray(second), rows, preferred_element_type=jnp.float32
    )
    parts = parts.reshape(count_img, 2, L, L // BLK, BLK)
    blocks = jnp.transpose(parts, (0, 2, 3, 1, 4))
    return blocks.reshape(count_img * PB, 2 * BLK).astype(jnp.bfloat16)


def ctf_rows(block_id, focus):
    row_id = block_id // (L // BLK)
    col_id = block_id % (L // BLK) * BLK
    lane_ids = jnp.arange(BLK, dtype=jnp.int32)
    freq_y = (row_id - L // 2).astype(jnp.float32) / L
    freq_x = (col_id[..., None] + lane_ids - L // 2).astype(jnp.float32) / L
    radius = freq_x * freq_x + (freq_y * freq_y)[..., None]
    return -jnp.sin(math.pi * focus.astype(jnp.float32)[..., None] * radius + phase_shift)


def residual_terms(prediction, observed, ctf_values, live_slots):
    shape = prediction.shape
    pred_wide = prediction.astype(jnp.float32).reshape(shape[:-1] + (2, BLK))
    obs_wide = observed.astype(jnp.float32).reshape(shape[:-1] + (2, BLK))
    factor = ctf_values[..., None, :]
    misfit = factor * (factor * pred_wide - obs_wide)
    misfit = jnp.where(live_slots[..., None, None], misfit, 0.0)
    return misfit.reshape(shape).astype(jnp.bfloat16)


def tap_matrix_t(tap_ids, weights, block_count):
    owners, taps, slots = tap_ids.shape
    flat_taps = jnp.transpose(tap_ids, (1, 0, 2)).reshape(taps, owners * slots)
    flat_weights = jnp.transpose(weights, (1, 0, 2)).reshape(taps, owners * slots)
    block_ids = jnp.arange(block_count, dtype=jnp.int32)
    picked = jnp.where(
        flat_taps[:, None, :] == block_ids[None, :, None],
        flat_weights[:, None, :],
        jnp.zeros((), jnp.bfloat16),
    )
    return jnp.sum(picked, axis=0, dtype=jnp.bfloat16)


def split_whole(values):
    return (values // 256).astype(jnp.bfloat16), (values % 256).astype(jnp.bfloat16)


def meta_kernel(counts_ref, taps_ref, weights_ref, pixel_ref, focus_ref, out_ref):
    owners, taps, capacity = taps_ref.shape
    out_ref[:, 0:taps, :] = taps_ref[...].astype(jnp.float32)
    out_ref[:, taps : 2 * taps, :] = weights_ref[...].astype(jnp.float32)
    pixels = pixel_ref[...]
    image = pixels // PB
    focus_all = focus_ref[...].astype(jnp.float32)
    focus = jnp.zeros(pixels.shape, jnp.float32)
    for index in range(focus_all.shape[1]):
        focus = jnp.where(image == index, focus_all[:, index : index + 1], focus)
    block = (pixels % PB).astype(jnp.float32)
    lanes = lax.broadcasted_iota(jnp.int32, (1, capacity), 1)
    for owner in range(owners):
        out_ref[owner, 2 * taps : 2 * taps + 1, :] = block[owner : owner + 1]
        out_ref[owner, 2 * taps + 1 : 2 * taps + 2, :] = focus[owner : owner + 1]
        live = (lanes < counts_ref[owner]).astype(jnp.float32)
        out_ref[owner, 2 * taps + 2 : 2 * taps + 3, :] = live


def slot_meta(counts, tap_ids, weights, pixel_ids, defocus):
    owners, taps, capacity = tap_ids.shape
    vmem = pltpu.MemorySpace.VMEM
    return pl.pallas_call(
        meta_kernel,
        out_shape=jax.ShapeDtypeStruct((owners, 2 * taps + 3, capacity), jnp.float32),
        in_specs=[
            pl.BlockSpec(memory_space=pltpu.MemorySpace.SMEM),
            pl.BlockSpec(memory_space=vmem),
            pl.BlockSpec(memory_space=vmem),
            pl.BlockSpec(memory_space=vmem),
            pl.BlockSpec(memory_space=vmem),
        ],
        out_specs=pl.BlockSpec(memory_space=vmem),
    )(counts, tap_ids, weights, pixel_ids, defocus.reshape(1, -1))


def local(images, defocus, volume, counts, slot_pixel, slot_taps, slot_weights):
    first, second = dft_tables()
    extract = volume.astype(jnp.bfloat16)
    width = volume.shape[1]
    slot_count = counts[0, 0]
    pixel_ids = slot_pixel[0, 0]
    tap_ids = slot_taps[0, 0]
    weights = slot_weights[0, 0]
    owners, taps, capacity = tap_ids.shape
    meta = slot_meta(slot_count, tap_ids, weights, pixel_ids, defocus)
    got_meta = lax.all_to_all(meta, "vol", split_axis=0, concat_axis=0, tiled=True)
    observed = transform(images, first, second)
    flat_pixels = pixel_ids.reshape(-1)
    onehot = (flat_pixels[:, None] == jnp.arange(observed.shape[0], dtype=jnp.int32)[None, :])
    rows = jnp.dot(onehot.astype(jnp.bfloat16), observed, preferred_element_type=jnp.float32)
    rows = rows.astype(jnp.bfloat16).reshape(owners, capacity, width)
    got_rows = lax.all_to_all(rows, "vol", split_axis=0, concat_axis=0, tiled=True)
    got_taps = got_meta[:, :taps].astype(jnp.int32)
    got_weights = got_meta[:, taps : 2 * taps].astype(jnp.bfloat16)
    got_block = got_meta[:, 2 * taps].astype(jnp.int32)
    got_focus = got_meta[:, 2 * taps + 1]
    got_live = got_meta[:, 2 * taps + 2] > 0.5
    matrix_t = tap_matrix_t(got_taps, got_weights, volume.shape[0])
    prediction = lax.dot_general(
        matrix_t, extract, (((0,), (0,)), ((), ())), preferred_element_type=jnp.float32
    )
    prediction = prediction.astype(jnp.bfloat16).reshape(owners, capacity, -1)
    ctf_values = ctf_rows(got_block, got_focus)
    weighted = residual_terms(prediction, got_rows, ctf_values, got_live)
    flat_residual = weighted.reshape(-1, width)
    shards = lax.axis_size("ptcl")
    if shards == 4:
        me = lax.axis_index("ptcl")
        on_chip = [(i, i ^ 1) for i in range(shards)]
        across = [(i, i ^ 2) for i in range(shards)]
        half = matrix_t.shape[0] // 2
        core = me % 2
        for_sibling = jnp.dot(
            lax.dynamic_slice_in_dim(matrix_t, (1 - core) * half, half, axis=0),
            flat_residual,
            preferred_element_type=jnp.float32,
        )
        arrived = lax.ppermute(for_sibling, "ptcl", on_chip)
        own = jnp.dot(
            lax.dynamic_slice_in_dim(matrix_t, core * half, half, axis=0),
            flat_residual,
            preferred_element_type=jnp.float32,
        )
        mine = (own + arrived).astype(jnp.bfloat16)
        total = mine.astype(jnp.float32) + lax.ppermute(mine, "ptcl", across).astype(jnp.float32)
        updated = lax.dynamic_slice_in_dim(volume, core * half, half, axis=0) - learn_rate * total
        other = lax.ppermute(updated, "ptcl", on_chip)
        result = lax.dynamic_update_slice_in_dim(volume, updated, core * half, axis=0)
        return lax.dynamic_update_slice_in_dim(result, other, (1 - core) * half, axis=0)
    gradient = jnp.dot(matrix_t, flat_residual, preferred_element_type=jnp.float32)
    partial = gradient.astype(jnp.bfloat16)
    parts = partial.reshape(shards, -1, gradient.shape[1])
    got_parts = lax.all_to_all(parts, "ptcl", split_axis=0, concat_axis=0, tiled=True)
    part_sum = jnp.sum(got_parts.astype(jnp.float32), axis=0)
    rows_each = part_sum.shape[0]
    start = lax.axis_index("ptcl") * rows_each
    mine = lax.dynamic_slice_in_dim(volume, start, rows_each, axis=0)
    updated = mine - learn_rate * part_sum
    return lax.all_gather(updated, "ptcl", axis=0, tiled=True)


def solution(mesh):
    placed = (
        P(("vol", "ptcl"), None, None),
        P(("vol", "ptcl")),
        P("vol", None),
        P("vol", "ptcl", None),
        P("vol", "ptcl", None, None),
        P("vol", "ptcl", None, None, None),
        P("vol", "ptcl", None, None, None),
    )
    return jax.shard_map(
        local, mesh=mesh, in_specs=placed, out_specs=P("vol", None), check_vma=False
    )
```
